256 devices in a mesh: loop: 4 (over y), inner: 8 (over x, core), batch: 8 (over z).
Axes of the slice: x: 4, y: 4, z: 8, core: 2. Of those that a mesh axis runs over, the one named last changes fastest.
Arguments:
- tokens: bfloat16 [32768, 4096], P(('loop', 'inner', 'batch')), may hold values from -24 to 24
- block_ids: int32 [32768, 4], P(('loop', 'inner', 'batch')), may hold values from 0 to 127, all different within a row; in each aligned block of 128 rows (0 to 127, 128 to 255, ...) at most 5 rows name the same one
- latent_mask: int32 [32768, 4, 64], P(('loop', 'inner', 'batch')), may hold values 0 or 1
- enc_weight: bfloat16 [4096, 8192], P(None, ('loop', 'inner')), may hold values from -0.09375 to 0.09375
- enc_bias: bfloat16 [8192], P(('loop', 'inner')), may hold values from -3 to 3
- dec_weight: bfloat16 [8192, 4096], P(('loop', 'inner')), may hold values from -1 to 1
- dec_bias: bfloat16 [4096], replicated, may hold values from -5 to 5
Outputs:
- grad_enc_weight: float32 [4096, 8192], P('batch', ('loop', 'inner'))
- grad_enc_bias: float32 [8192], P(('loop', 'inner', 'batch'))
- grad_dec_weight: float32 [8192, 4096], P(('loop', 'inner'), 'batch')
The draws below stay inside these ranges and needn't reach their ends.
Inputs may be any that keep to these rules, and one draw needn't show every extreme that they name: `block_ids`: each row names 4 different blocks. Among the rows of one device no block is named more than 5 times, and some block is named exactly 5 times.
All inputs are finite; a program needn't handle non-finite values. No bound on the sum of `latent_mask` on one device may be relied on, other than what follows from the above.
Results may differ from the reference program's by a relative error of at most 0.015.
Values may be sent and summed in bfloat16 or wider, within the bound.
No kernel may reach another device: no remote copies, remote signals or barrier semaphores. Data moves between devices by JAX's collectives and lax.ppermute only.
A program may use at most 128 MiB of HBM per device.

```python
import math
import jax
import jax.numpy as jnp
import numpy as np
from jax import lax

D = 4096
BLK = 64
TOPB = 4
TOK_DEV = 128
NBLK = 128
LAT = 8192
TOKENS = 32768
CAP = 5
N_LOOP = 4
N_INNER = 8
N_BATCH = 8


def touch_ends(array, own_key, low, top_value):
    spot = [jax.random.randint(jax.random.fold_in(own_key, axis), (), 0, length) for axis, length in enumerate(array.shape)]
    main_axis = array.shape.index(max(array.shape))
    next_to = spot[:main_axis] + [(spot[main_axis] + 1) % array.shape[main_axis]] + spot[main_axis + 1:]
    return array.at[tuple(spot)].set(low).at[tuple(next_to)].set(top_value)


def raised(drawn, key, source, target, shards_of, factor):
    def block_of(axis_at):
        return (jnp.arange(drawn.shape[axis_at]) // (drawn.shape[axis_at] // shards_of)).reshape((-1,) + (1,) * (drawn.ndim - 1 - axis_at))

    first = jax.random.permutation(key, shards_of)[block_of(target)]
    far = (block_of(target) + shards_of // 2) % shards_of
    return jnp.where((block_of(source) == first) | (block_of(source) == far), factor * drawn, drawn)


def block_scale(key, dims, pieces, smallest, high):
    factor_of = 1.0
    for dim, shards_of in pieces:
        heights = jax.random.uniform(jax.random.fold_in(jax.random.fold_in(key, 6), dim), (shards_of,), jnp.float32, smallest / len(pieces), high / len(pieces))
        factor_of = factor_of * jnp.repeat(jnp.exp(heights), dims[dim] // shards_of).reshape((-1,) + (1,) * (len(dims) - 1 - dim))
    return factor_of


def deal_out(own_key, own, number, rows, number_of, top, limit, skew):
    order = jax.random.permutation(own_key, number_of)
    packed, usual = load_shares(number_of, rows * top, limit, skew, True), load_shares(number_of, rows * top, limit, skew, False)
    places = jnp.arange(number_of)

    def named(sizes, rotation):
        used = int((sizes > 0).sum())
        fixed = max(1, used // 4)
        moved = fixed + (places - fixed + rotation * (used - fixed)) % max(1, number_of - fixed)
        return jnp.zeros((number_of,), jnp.int32).at[order[jnp.where(places < fixed, places, moved)]].set(jnp.asarray(sizes, jnp.int32))

    sizes = jnp.where(number % 4 == 0, named(packed, number // 4), named(usual, number - number // 4 - 1))
    mixed = jax.random.permutation(jax.random.fold_in(own, 3), number_of)
    source_of, receiver = mixed[0:number_of // 2 * 2:2], mixed[1:number_of // 2 * 2:2]
    margin = jnp.minimum(sizes[source_of] - 1, limit - sizes[receiver]) // 2
    margin = jnp.where((source_of == order[0]) | (receiver == order[0]) | (sizes[receiver] == 0), 0, jnp.maximum(margin, 0))
    moved = jax.random.randint(jax.random.fold_in(own, 4), (number_of // 2,), 0, 1 << 20) % (margin + 1)
    sizes = sizes.at[source_of].add(-moved).at[receiver].add(moved)
    labels = jnp.searchsorted(jnp.cumsum(sizes), jnp.arange(rows * top), side="right").astype(jnp.int32)
    table = labels.reshape(top, rows).T
    table = table[jax.random.permutation(jax.random.fold_in(own, 1), rows)]
    rotation = jax.random.randint(jax.random.fold_in(own, 2), (rows, 1), 0, top)
    return jnp.take_along_axis(table, (jnp.arange(top)[None, :] + rotation) % top, axis=1)


def load_shares(number_of, total, bound, skew, full):
    portions = [(1 << 20) // math.isqrt(standing ** skew) + 1 for standing in range(1, number_of + 1)]
    largest = bound if full else min(bound, max(-(-total // number_of), total * portions[0] // sum(portions)))
    least = 1 if total - largest >= number_of - 1 else 0
    given, spare = [largest] + [least] * (number_of - 1), total - largest - least * (number_of - 1)
    while spare > 0:
        candidates = [i for i in range(1, number_of) if given[i] < largest] or [i for i in range(1, number_of) if given[i] < bound]
        mass, left = sum([portions[i] for i in candidates]), spare
        for i in candidates:
            more = min(bound - given[i], max(1, left * portions[i] // mass), spare)
            given[i] = given[i] + more
            spare = spare - more
    return np.array(given)


def bell_draw(key, shape, width, most, pieces=(), kind=jnp.bfloat16):
    values = width * jax.random.normal(key, shape, jnp.float32)
    if pieces:
        values = values * block_scale(key, shape, pieces, -0.22, 0.18)
    return jnp.clip(values, -most, most).astype(kind)


def gaussian_with(stream_key, shape, scale, limit, cuts, heavy, kind=jnp.bfloat16):
    values = scale * jax.random.normal(stream_key, shape, jnp.float32)
    if cuts:
        values = values * block_scale(stream_key, shape, cuts, -0.22, 0.18)
    return jnp.clip(raised(values, jax.random.fold_in(stream_key, 3), *heavy), -limit, limit).astype(kind)


def setup_inputs(seed: int = 0) -> dict:
    splits = jax.random.split(jax.random.key(seed), 8)
    tokens = gaussian_with(splits[0], (TOKENS, D), 1.0, 24.0, ((0, 256),), (0, 1, 256, 6.0))
    block_ids_keys = jax.random.split(jax.random.fold_in(splits[1], 1), TOKENS // TOK_DEV)
    block_ids_turns = jax.random.permutation(jax.random.fold_in(splits[1], 3), TOKENS // TOK_DEV)
    block_ids = jax.vmap(lambda own, number: deal_out(jax.random.fold_in(splits[1], 2), own, number, TOK_DEV, NBLK, TOPB, CAP, 2))(block_ids_keys, block_ids_turns).reshape((TOKENS, TOPB))
    latent_mask = touch_ends((jax.random.randint(splits[2], (TOKENS, TOPB, BLK), 0, 8) < 1).astype(jnp.int32), jax.random.fold_in(splits[2], 1), 0, 1)
    enc_weight = bell_draw(splits[3], (D, LAT), D ** -0.5, 0.09375, ((1, 32),))
    enc_bias = bell_draw(splits[4], (LAT,), 0.5, 3.0, ((0, 32),))
    dec_weight = bell_draw(splits[5], (LAT, D), (TOPB * BLK // 8) ** -0.5, 1.0, ((0, 32),))
    dec_bias = bell_draw(splits[6], (D,), 1.0, 5.0)
    return {"tokens": tokens, "block_ids": block_ids, "latent_mask": latent_mask, "enc_weight": enc_weight, "enc_bias": enc_bias, "dec_weight": dec_weight, "dec_bias": dec_bias}


def reference(tokens, block_ids, latent_mask, enc_weight, enc_bias, dec_weight, dec_bias):
    seg_len = N_LOOP * N_INNER * CAP
    routed = TOKENS * TOPB
    flat_ids = block_ids.reshape(-1).astype(jnp.int32)
    token_of = (jnp.arange(routed, dtype=jnp.int32) // TOPB).astype(jnp.int32)
    batch_of = ((token_of // TOK_DEV) % N_BATCH).astype(jnp.int32)
    seg_keys = (flat_ids * N_BATCH + batch_of).astype(jnp.int32)
    sorted_row_order = jnp.argsort(seg_keys, stable=True).astype(jnp.int32)
    counts = jax.ops.segment_sum(jnp.ones((routed,), jnp.int32), seg_keys, num_segments=NBLK * N_BATCH).astype(jnp.int32)
    starts = (jnp.cumsum(counts) - counts).astype(jnp.int32)
    order_pad = jnp.concatenate([sorted_row_order, jnp.zeros((seg_len,), jnp.int32)])
    mask_rows = latent_mask.reshape(routed, BLK)
    positions = jnp.arange(seg_len, dtype=jnp.int32)

    def segment(segment_key):
        seg_start = starts[segment_key].astype(jnp.int32)
        live_slot = positions < counts[segment_key]
        row_at = lax.dynamic_slice(order_pad, (seg_start,), (seg_len,))
        row_at = jnp.where(live_slot, row_at, 0).astype(jnp.int32)
        token_at = (row_at // TOPB).astype(jnp.int32)
        latent_gate = jnp.where(live_slot[:, None], mask_rows[row_at], 0).astype(jnp.float32)
        first = ((segment_key // N_BATCH) * BLK).astype(jnp.int32)
        zero_idx = jnp.zeros((), jnp.int32)
        enc_block = lax.dynamic_slice(enc_weight, (zero_idx, first), (D, BLK))
        bias_block = lax.dynamic_slice(enc_bias, (first,), (BLK,))
        dec_block = lax.dynamic_slice(dec_weight, (first, zero_idx), (BLK, D))
        slot_rows = tokens[token_at]
        preact = jnp.dot(slot_rows, enc_block, preferred_element_type=jnp.float32) + bias_block.astype(jnp.float32)
        sparse_latent_code = (preact * latent_gate).astype(jnp.bfloat16)
        return token_at, latent_gate, slot_rows, sparse_latent_code, dec_block

    def forward(rebuilt, segment_key):
        token_at, latent_gate, slot_rows, sparse_latent_code, dec_block = segment(segment_key)
        partial_value = jnp.dot(sparse_latent_code, dec_block, preferred_element_type=jnp.float32).astype(jnp.bfloat16)
        return rebuilt.at[token_at].add(partial_value.astype(jnp.float32)), None

    all_keys = jnp.arange(NBLK * N_BATCH, dtype=jnp.int32)
    rebuilt, _ = lax.scan(forward, jnp.zeros((TOKENS, D), jnp.float32), all_keys)
    residual_err = rebuilt + dec_bias.astype(jnp.float32) - tokens.astype(jnp.float32)
    err_b = residual_err.astype(jnp.bfloat16)

    def backward_group(segment_key):
        token_at, latent_gate, slot_rows, sparse_latent_code, dec_block = segment(segment_key)
        error_rows_local = err_b[token_at]
        pre_grad = jnp.dot(error_rows_local, dec_block.T, preferred_element_type=jnp.float32) * latent_gate
        pre_grad_b = pre_grad.astype(jnp.bfloat16)
        enc_part = jnp.dot(slot_rows.T, pre_grad_b, preferred_element_type=jnp.float32).astype(jnp.bfloat16)
        dec_part = jnp.dot(sparse_latent_code.T, error_rows_local, preferred_element_type=jnp.float32).astype(jnp.bfloat16)
        bias_part = jnp.sum(pre_grad, axis=0).astype(jnp.bfloat16)
        return enc_part, dec_part, bias_part

    def backward_block(block_id):
        enc_total = jnp.zeros((D, BLK), jnp.float32)
        dec_total = jnp.zeros((BLK, D), jnp.float32)
        bias_total = jnp.zeros((BLK,), jnp.float32)
        for group in range(N_BATCH):
            enc_part, dec_part, bias_part = backward_group((block_id * N_BATCH + group).astype(jnp.int32))
            enc_total = enc_total + enc_part.astype(jnp.float32)
            dec_total = dec_total + dec_part.astype(jnp.float32)
            bias_total = bias_total + bias_part.astype(jnp.float32)
        return enc_total, dec_total, bias_total

    enc_all, dec_all, bias_all = lax.map(backward_block, jnp.arange(NBLK, dtype=jnp.int32))
    grad_enc_weight = jnp.transpose(enc_all, (1, 0, 2)).reshape(D, LAT)
    grad_dec_weight = dec_all.reshape(LAT, D)
    grad_enc_bias = bias_all.reshape(LAT)
    return (grad_enc_weight, grad_enc_bias, grad_dec_weight)
```

```python
import jax
import jax.numpy as jnp
from jax import lax
from jax.sharding import PartitionSpec as P

BLK = 64
OWNER_AXES = ("loop", "inner")


def exchange(rows):
    return lax.all_to_all(rows, OWNER_AXES, split_axis=0, concat_axis=0, tiled=True)


def pick_rows(select, rows):
    return lax.dot_general(
        select, rows, (((0,), (0,)), ((), ())), preferred_element_type=jnp.float32
    ).astype(rows.dtype)


def shards(tokens, block_ids, latent_mask, enc_weight, enc_bias, dec_weight, dec_bias):
    tok_dev, model_width = tokens.shape
    pick_count = block_ids.shape[1]
    local_lat = enc_weight.shape[1]
    local_blocks = local_lat // BLK
    owners = lax.axis_size("loop") * lax.axis_size("inner")
    num_blocks = local_blocks * owners
    n_batch = lax.axis_size("batch")
    capacity = (9 * tok_dev * pick_count + 8 * num_blocks - 1) // (8 * num_blocks)
    slot_count = num_blocks * capacity
    routed = tok_dev * pick_count

    with jax.named_scope("slot_tables"):
        flat_ids = block_ids.reshape(routed)
        row_pos = jnp.arange(routed, dtype=jnp.int32)
        earlier_same = (flat_ids[:, None] == flat_ids[None, :]) & (row_pos[None, :] < row_pos[:, None])
        slot_rank = jnp.sum(earlier_same.astype(jnp.int32), axis=1)
        target = flat_ids * capacity + slot_rank
        row_to_slot = target[:, None] == jnp.arange(slot_count, dtype=jnp.int32)[None, :]
        row_to_slot = row_to_slot.astype(jnp.bfloat16)
        token_to_slot = jnp.sum(
            row_to_slot.reshape(tok_dev, pick_count, slot_count), axis=1
        ).astype(jnp.bfloat16)

    with jax.named_scope("dispatch"):
        send_rows = pick_rows(token_to_slot, tokens)
        mask_rows = latent_mask.reshape(routed, BLK).astype(jnp.bfloat16)
        send_mask = pick_rows(row_to_slot, mask_rows)
        slot_rows = exchange(send_rows)
        got_mask = exchange(send_mask)

    with jax.named_scope("encode_decode"):
        slot_block = (jnp.arange(slot_count, dtype=jnp.int32) // capacity) % local_blocks
        col_block = jnp.arange(local_lat, dtype=jnp.int32) // BLK
        in_block = slot_block[:, None] == col_block[None, :]
        latent_gate = jnp.where(
            in_block, jnp.tile(got_mask.astype(jnp.float32), (1, local_blocks)), 0.0
        )
        preact = jnp.dot(slot_rows, enc_weight, preferred_element_type=jnp.float32)
        preact = preact + enc_bias.astype(jnp.float32)[None, :]
        sparse_latent_code = (preact * latent_gate).astype(jnp.bfloat16)
        partials = jnp.dot(
            sparse_latent_code, dec_weight, preferred_element_type=jnp.float32
        ).astype(jnp.bfloat16)

    with jax.named_scope("combine"):
        returned = exchange(partials)
        rebuilt = jnp.dot(token_to_slot, returned, preferred_element_type=jnp.float32)
        residual_err = rebuilt + dec_bias.astype(jnp.float32)[None, :] - tokens.astype(jnp.float32)
        err_b = residual_err.astype(jnp.bfloat16)
        send_err = pick_rows(token_to_slot, err_b)
        error_rows = exchange(send_err)

    with jax.named_scope("backward"):
        pre_grad = lax.dot_general(
            error_rows, dec_weight, (((1,), (1,)), ((), ())), preferred_element_type=jnp.float32
        ) * latent_gate
        pre_grad_b = pre_grad.astype(jnp.bfloat16)
        enc_grad = lax.dot_general(
            slot_rows, pre_grad_b, (((0,), (0,)), ((), ())), preferred_element_type=jnp.float32
        )
        dec_grad_t = lax.dot_general(
            error_rows, sparse_latent_code, (((0,), (0,)), ((), ())),
            preferred_element_type=jnp.float32,
        )
        bias_grad = jnp.sum(pre_grad, axis=0)

    with jax.named_scope("grad_reduce"):
        rows_per = model_width // n_batch
        bias_per = local_lat // n_batch
        pad_rows = 16
        weights = jnp.concatenate(
            [
                enc_grad.astype(jnp.bfloat16).reshape(n_batch, rows_per, local_lat),
                dec_grad_t.astype(jnp.bfloat16).reshape(n_batch, rows_per, local_lat),
            ],
            axis=2,
        )
        bias_block = jnp.pad(
            bias_grad.astype(jnp.bfloat16).reshape(n_batch, 1, bias_per),
            ((0, 0), (0, pad_rows - 1), (0, 2 * local_lat - bias_per)),
        )
        stacked = jnp.concatenate([weights, bias_block], axis=1).reshape(
            n_batch * (rows_per + pad_rows), 2 * local_lat
        )
        reduced = lax.psum_scatter(stacked, "batch", scatter_dimension=0, tiled=True).astype(
            jnp.float32
        )
        grad_enc_weight = reduced[:rows_per, :local_lat]
        grad_dec_weight = reduced[:rows_per, local_lat:].T
        bias_share = reduced[rows_per, :bias_per]
    return (grad_enc_weight, bias_share, grad_dec_weight)


def solution(mesh):
    in_specs = (
        P(("loop", "inner", "batch"), None),
        P(("loop", "inner", "batch"), None),
        P(("loop", "inner", "batch"), None, None),
        P(None, ("loop", "inner")),
        P(("loop", "inner")),
        P(("loop", "inner"), None),
        P(),
    )
    out_specs = (
        P("batch", ("loop", "inner")),
        P(("loop", "inner", "batch")),
        P(("loop", "inner"), "batch"),
    )
    return jax.shard_map(shards, mesh=mesh, in_specs=in_specs, out_specs=out_specs, check_vma=False)
```

```python
import jax
import jax.numpy as jnp
from jax import lax
from jax.sharding import PartitionSpec as P

BLK = 64
OWNER_AXES = ("loop", "inner")


def exchange(rows):
    return lax.all_to_all(rows, OWNER_AXES, split_axis=0, concat_axis=0, tiled=True)


def pick_rows(select, rows):
    return lax.dot_general(
        select, rows, (((0,), (0,)), ((), ())), preferred_element_type=jnp.float32
    ).astype(rows.dtype)


def shards(tokens, block_ids, latent_mask, enc_weight, enc_bias, dec_weight, dec_bias):
    tok_dev, model_width = tokens.shape
    pick_count = block_ids.shape[1]
    local_lat = enc_weight.shape[1]
    local_blocks = local_lat // BLK
    owners = lax.axis_size("loop") * lax.axis_size("inner")
    num_blocks = local_blocks * owners
    n_batch = lax.axis_size("batch")
    capacity = (9 * tok_dev * pick_count + 8 * num_blocks - 1) // (8 * num_blocks)
    slot_count = num_blocks * capacity
    routed = tok_dev * pick_count

    with jax.named_scope("slot_tables"):
        flat_ids = block_ids.reshape(routed)
        row_pos = jnp.arange(routed, dtype=jnp.int32)
        earlier_same = (flat_ids[:, None] == flat_ids[None, :]) & (row_pos[None, :] < row_pos[:, None])
        slot_rank = jnp.sum(earlier_same.astype(jnp.int32), axis=1)
        target = ((flat_ids // local_blocks) * capacity + slot_rank) * local_blocks + flat_ids % local_blocks
        row_to_slot = target[:, None] == jnp.arange(slot_count, dtype=jnp.int32)[None, :]
        row_to_slot = row_to_slot.astype(jnp.bfloat16)
        token_to_slot = jnp.sum(
            row_to_slot.reshape(tok_dev, pick_count, slot_count), axis=1
        ).astype(jnp.bfloat16)
        groups = slot_count // local_blocks
        token_to_group = token_to_slot.reshape(tok_dev, groups, local_blocks)

    with jax.named_scope("dispatch"):
        send_rows = pick_rows(token_to_group, tokens)
        mask_rows = latent_mask.reshape(routed, BLK).astype(jnp.bfloat16)
        send_mask = pick_rows(row_to_slot, mask_rows)
        slot_rows = exchange(send_rows)
        got_mask = exchange(send_mask).reshape(groups, local_blocks, BLK)

    with jax.named_scope("encode_decode"):
        slot_block = jnp.arange(local_blocks, dtype=jnp.int32)
        col_block = jnp.arange(local_lat, dtype=jnp.int32) // BLK
        in_block = slot_block[:, None] == col_block[None, :]
        latent_gate = jnp.where(
            in_block[None], jnp.tile(got_mask.astype(jnp.float32), (1, 1, local_blocks)), 0.0
        )
        preact = lax.dot_general(
            slot_rows, enc_weight, (((2,), (0,)), ((), ())), preferred_element_type=jnp.float32
        )
        preact = preact + enc_bias.astype(jnp.float32)[None, None, :]
        sparse_latent_code = (preact * latent_gate).astype(jnp.bfloat16)
        partials = lax.dot_general(
            sparse_latent_code, dec_weight, (((2,), (0,)), ((), ())),
            preferred_element_type=jnp.float32,
        ).astype(jnp.bfloat16)

    with jax.named_scope("combine"):
        returned = exchange(partials)
        rebuilt = lax.dot_general(
            token_to_group, returned, (((1, 2), (0, 1)), ((), ())),
            preferred_element_type=jnp.float32,
        )
        residual_err = rebuilt + dec_bias.astype(jnp.float32)[None, :] - tokens.astype(jnp.float32)
        err_b = residual_err.astype(jnp.bfloat16)
        send_err = pick_rows(token_to_group, err_b)
        error_rows = exchange(send_err)

    with jax.named_scope("backward"):
        pre_grad = lax.dot_general(
            error_rows, dec_weight, (((2,), (1,)), ((), ())), preferred_element_type=jnp.float32
        ) * latent_gate
        pre_grad_b = pre_grad.astype(jnp.bfloat16)
        enc_grad = lax.dot_general(
            slot_rows, pre_grad_b, (((0, 1), (0, 1)), ((), ())), preferred_element_type=jnp.float32
        )
        dec_grad_t = lax.dot_general(
            error_rows, sparse_latent_code, (((0, 1), (0, 1)), ((), ())),
            preferred_element_type=jnp.float32,
        )
        bias_grad = jnp.sum(pre_grad, axis=(0, 1))

    with jax.named_scope("grad_reduce"):
        rows_per = model_width // n_batch
        bias_per = local_lat // n_batch
        pad_rows = 16
        weights = jnp.concatenate(
            [
                enc_grad.astype(jnp.bfloat16).reshape(n_batch, rows_per, local_lat),
                dec_grad_t.astype(jnp.bfloat16).reshape(n_batch, rows_per, local_lat),
            ],
            axis=2,
        )
        bias_block = jnp.pad(
            bias_grad.astype(jnp.bfloat16).reshape(n_batch, 1, bias_per),
            ((0, 0), (0, pad_rows - 1), (0, 2 * local_lat - bias_per)),
        )
        stacked = jnp.concatenate([weights, bias_block], axis=1).reshape(
            n_batch * (rows_per + pad_rows), 2 * local_lat
        )
        reduced = lax.psum_scatter(stacked, "batch", scatter_dimension=0, tiled=True).astype(
            jnp.float32
        )
        grad_enc_weight = reduced[:rows_per, :local_lat]
        grad_dec_weight = reduced[:rows_per, local_lat:].T
        bias_share = reduced[rows_per, :bias_per]
    return (grad_enc_weight, bias_share, grad_dec_weight)


def solution(mesh):
    in_specs = (
        P(("loop", "inner", "batch"), None),
        P(("loop", "inner", "batch"), None),
        P(("loop", "inner", "batch"), None, None),
        P(None, ("loop", "inner")),
        P(("loop", "inner")),
        P(("loop", "inner"), None),
        P(),
    )
    out_specs = (
        P("batch", ("loop", "inner")),
        P(("loop", "inner", "batch")),
        P(("loop", "inner"), "batch"),
    )
    return jax.shard_map(shards, mesh=mesh, in_specs=in_specs, out_specs=out_specs, check_vma=False)
```

```python
import jax
import jax.numpy as jnp
from jax import lax
from jax.sharding import PartitionSpec as P

BLK = 64
OWNER_AXES = ("loop", "inner")


def exchange(rows):
    return lax.all_to_all(rows, OWNER_AXES, split_axis=0, concat_axis=0, tiled=True)


def pick_rows(select, rows):
    return lax.dot_general(
        select, rows, (((0,), (0,)), ((), ())), preferred_element_type=jnp.float32
    ).astype(rows.dtype)


def shards(tokens, block_ids, latent_mask, enc_weight, enc_bias, dec_weight, dec_bias):
    tok_dev, model_width = tokens.shape
    pick_count = block_ids.shape[1]
    local_lat = enc_weight.shape[1]
    local_blocks = local_lat // BLK
    owners = lax.axis_size("loop") * lax.axis_size("inner")
    num_blocks = local_blocks * owners
    n_batch = lax.axis_size("batch")
    capacity = (9 * tok_dev * pick_count + 8 * num_blocks - 1) // (8 * num_blocks)
    slot_count = num_blocks * capacity
    routed = tok_dev * pick_count

    with jax.named_scope("slot_tables"):
        flat_ids = block_ids.reshape(routed)
        row_pos = jnp.arange(routed, dtype=jnp.int32)
        earlier_same = (flat_ids[:, None] == flat_ids[None, :]) & (row_pos[None, :] < row_pos[:, None])
        slot_rank = jnp.sum(earlier_same.astype(jnp.int32), axis=1)
        target = ((flat_ids // local_blocks) * capacity + slot_rank) * local_blocks + flat_ids % local_blocks
        row_to_slot = target[:, None] == jnp.arange(slot_count, dtype=jnp.int32)[None, :]
        row_to_slot = row_to_slot.astype(jnp.bfloat16)
        token_to_slot = jnp.sum(
            row_to_slot.reshape(tok_dev, pick_count, slot_count), axis=1
        ).astype(jnp.bfloat16)
        groups = slot_count // local_blocks
        token_to_group = token_to_slot.reshape(tok_dev, groups, local_blocks)

    chunks = 2
    chunk_blocks = local_blocks // chunks
    chunk_lat = chunk_blocks * BLK
    rows_per = model_width // n_batch
    bias_per = local_lat // n_batch
    pad_rows = 16

    with jax.named_scope("dispatch"):
        mask_rows = latent_mask.reshape(routed, BLK).astype(jnp.bfloat16)
        send_mask = pick_rows(row_to_slot, mask_rows)
        got_mask = exchange(send_mask).reshape(groups, local_blocks, BLK).astype(jnp.float32)
        select = [token_to_group[:, :, c * chunk_blocks:(c + 1) * chunk_blocks] for c in range(chunks)]
        slot_rows = [exchange(pick_rows(select[c], tokens)) for c in range(chunks)]

    with jax.named_scope("encode_decode"):
        slot_block = jnp.arange(chunk_blocks, dtype=jnp.int32)
        col_block = jnp.arange(chunk_lat, dtype=jnp.int32) // BLK
        in_block = (slot_block[:, None] == col_block[None, :])[None]
        gates, codes, returned = [], [], []
        for c in range(chunks):
            lat = slice(c * chunk_lat, (c + 1) * chunk_lat)
            mask_c = got_mask[:, c * chunk_blocks:(c + 1) * chunk_blocks, :]
            gate_c = jnp.where(in_block, jnp.tile(mask_c, (1, 1, chunk_blocks)), 0.0)
            preact = lax.dot_general(
                slot_rows[c], enc_weight[:, lat], (((2,), (0,)), ((), ())),
                preferred_element_type=jnp.float32,
            )
            preact = preact + enc_bias[lat].astype(jnp.float32)[None, None, :]
            code_c = (preact * gate_c).astype(jnp.bfloat16)
            partials = lax.dot_general(
                code_c, dec_weight[lat, :], (((2,), (0,)), ((), ())),
                preferred_element_type=jnp.float32,
            ).astype(jnp.bfloat16)
            gates.append(gate_c)
            codes.append(code_c)
            returned.append(exchange(partials))

    with jax.named_scope("combine"):
        rebuilt = dec_bias.astype(jnp.float32)[None, :] - tokens.astype(jnp.float32)
        for c in range(chunks):
            rebuilt = rebuilt + lax.dot_general(
                select[c], returned[c], (((1, 2), (0, 1)), ((), ())),
                preferred_element_type=jnp.float32,
            )
        err_b = rebuilt.astype(jnp.bfloat16)
        error_rows = [exchange(pick_rows(select[c], err_b)) for c in range(chunks)]

    with jax.named_scope("backward"):
        reduced, bias_parts = [], []
        for c in range(chunks):
            lat = slice(c * chunk_lat, (c + 1) * chunk_lat)
            pre_grad = lax.dot_general(
                error_rows[c], dec_weight[lat, :], (((2,), (1,)), ((), ())),
                preferred_element_type=jnp.float32,
            ) * gates[c]
            pre_grad_b = pre_grad.astype(jnp.bfloat16)
            enc_grad = lax.dot_general(
                slot_rows[c], pre_grad_b, (((0, 1), (0, 1)), ((), ())),
                preferred_element_type=jnp.float32,
            )
            dec_grad_t = lax.dot_general(
                error_rows[c], codes[c], (((0, 1), (0, 1)), ((), ())),
                preferred_element_type=jnp.float32,
            )
            bias_parts.append(jnp.sum(pre_grad, axis=(0, 1)))
            stacked = jnp.concatenate(
                [
                    enc_grad.astype(jnp.bfloat16).reshape(n_batch, rows_per, chunk_lat),
                    dec_grad_t.astype(jnp.bfloat16).reshape(n_batch, rows_per, chunk_lat),
                ],
                axis=2,
            )
            if c == chunks - 1:
                bias_grad = jnp.concatenate(bias_parts)
                bias_block = jnp.pad(
                    bias_grad.astype(jnp.bfloat16).reshape(n_batch, 1, bias_per),
                    ((0, 0), (0, pad_rows - 1), (0, 2 * chunk_lat - bias_per)),
                )
                stacked = jnp.concatenate([stacked, bias_block], axis=1)
            stacked = stacked.reshape(-1, 2 * chunk_lat)
            reduced.append(
                lax.psum_scatter(stacked, "batch", scatter_dimension=0, tiled=True).astype(
                    jnp.float32
                )
            )

    with jax.named_scope("grad_reduce"):
        grad_enc_weight = jnp.concatenate([r[:rows_per, :chunk_lat] for r in reduced], axis=1)
        grad_dec_weight = jnp.concatenate(
            [r[:rows_per, chunk_lat:] for r in reduced], axis=1
        ).T
        bias_share = reduced[-1][rows_per, :bias_per]
    return (grad_enc_weight, bias_share, grad_dec_weight)


def solution(mesh):
    in_specs = (
        P(("loop", "inner", "batch"), None),
        P(("loop", "inner", "batch"), None),
        P(("loop", "inner", "batch"), None, None),
        P(None, ("loop", "inner")),
        P(("loop", "inner")),
        P(("loop", "inner"), None),
        P(),
    )
    out_specs = (
        P("batch", ("loop", "inner")),
        P(("loop", "inner", "batch")),
        P(("loop", "inner"), "batch"),
    )
    return jax.shard_map(shards, mesh=mesh, in_specs=in_specs, out_specs=out_specs, check_vma=False)
```

```python
import jax
import jax.numpy as jnp
from jax import lax
from jax.sharding import PartitionSpec as P

BLK = 64
OWNER_AXES = ("loop", "inner")


def exchange(rows):
    return lax.all_to_all(rows, OWNER_AXES, split_axis=0, concat_axis=0, tiled=True)


def pick_rows(select, rows):
    return lax.dot_general(
        select, rows, (((0,), (0,)), ((), ())), preferred_element_type=jnp.float32
    ).astype(rows.dtype)


def shards(tokens, block_ids, latent_mask, enc_weight, enc_bias, dec_weight, dec_bias):
    tok_dev, model_width = tokens.shape
    pick_count = block_ids.shape[1]
    local_lat = enc_weight.shape[1]
    local_blocks = local_lat // BLK
    owners = lax.axis_size("loop") * lax.axis_size("inner")
    num_blocks = local_blocks * owners
    n_batch = lax.axis_size("batch")
    capacity = (9 * tok_dev * pick_count + 8 * num_blocks - 1) // (8 * num_blocks)
    slot_count = num_blocks * capacity
    routed = tok_dev * pick_count

    with jax.named_scope("slot_tables"):
        flat_ids = block_ids.reshape(routed)
        row_pos = jnp.arange(routed, dtype=jnp.int32)
        earlier_same = (flat_ids[:, None] == flat_ids[None, :]) & (row_pos[None, :] < row_pos[:, None])
        slot_rank = jnp.sum(earlier_same.astype(jnp.int32), axis=1)
        target = ((flat_ids // local_blocks) * capacity + slot_rank) * local_blocks + flat_ids % local_blocks
        row_to_slot = target[:, None] == jnp.arange(slot_count, dtype=jnp.int32)[None, :]
        row_to_slot = row_to_slot.astype(jnp.bfloat16)
        token_to_slot = jnp.sum(
            row_to_slot.reshape(tok_dev, pick_count, slot_count), axis=1
        ).astype(jnp.bfloat16)
        groups = slot_count // local_blocks
        token_to_group = token_to_slot.reshape(tok_dev, groups, local_blocks)

    chunks = 2
    chunk_blocks = local_blocks // chunks
    chunk_lat = chunk_blocks * BLK
    rows_per = model_width // n_batch
    bias_per = local_lat // n_batch
    pad_rows = 16

    with jax.named_scope("dispatch"):
        mask_rows = latent_mask.reshape(routed, BLK).astype(jnp.bfloat16)
        send_mask = pick_rows(row_to_slot, mask_rows)
        got_mask = exchange(send_mask).reshape(groups, local_blocks, BLK).astype(jnp.float32)
        all_rows = exchange(pick_rows(token_to_group, tokens))

    with jax.named_scope("encode_decode"):
        slot_block = jnp.arange(local_blocks, dtype=jnp.int32)
        col_block = jnp.arange(local_lat, dtype=jnp.int32) // BLK
        in_block = (slot_block[:, None] == col_block[None, :])[None]
        gate_all = jnp.where(in_block, jnp.tile(got_mask, (1, 1, local_blocks)), 0.0)
        preact = lax.dot_general(
            all_rows, enc_weight, (((2,), (0,)), ((), ())), preferred_element_type=jnp.float32
        )
        preact = preact + enc_bias.astype(jnp.float32)[None, None, :]
        code_all = (preact * gate_all).astype(jnp.bfloat16)
        partials = lax.dot_general(
            code_all, dec_weight, (((2,), (0,)), ((), ())), preferred_element_type=jnp.float32
        ).astype(jnp.bfloat16)
        returned = exchange(partials)

    with jax.named_scope("combine"):
        rebuilt = lax.dot_general(
            token_to_group, returned, (((1, 2), (0, 1)), ((), ())),
            preferred_element_type=jnp.float32,
        )
        rebuilt = rebuilt + dec_bias.astype(jnp.float32)[None, :] - tokens.astype(jnp.float32)
        err_b = rebuilt.astype(jnp.bfloat16)
        select = [token_to_group[:, :, c * chunk_blocks:(c + 1) * chunk_blocks] for c in range(chunks)]
        error_rows = [exchange(pick_rows(select[c], err_b)) for c in range(chunks)]
        part = [slice(c * chunk_blocks, (c + 1) * chunk_blocks) for c in range(chunks)]
        lats = [slice(c * chunk_lat, (c + 1) * chunk_lat) for c in range(chunks)]
        slot_rows = [all_rows[:, part[c], :] for c in range(chunks)]
        gates = [gate_all[:, part[c], lats[c]] for c in range(chunks)]
        codes = [code_all[:, part[c], lats[c]] for c in range(chunks)]

    with jax.named_scope("backward"):
        reduced, bias_parts = [], []
        for c in range(chunks):
            lat = slice(c * chunk_lat, (c + 1) * chunk_lat)
            pre_grad = lax.dot_general(
                error_rows[c], dec_weight[lat, :], (((2,), (1,)), ((), ())),
                preferred_element_type=jnp.float32,
            ) * gates[c]
            pre_grad_b = pre_grad.astype(jnp.bfloat16)
            enc_grad = lax.dot_general(
                slot_rows[c], pre_grad_b, (((0, 1), (0, 1)), ((), ())),
                preferred_element_type=jnp.float32,
            )
            dec_grad_t = lax.dot_general(
                error_rows[c], codes[c], (((0, 1), (0, 1)), ((), ())),
                preferred_element_type=jnp.float32,
            )
            bias_parts.append(jnp.sum(pre_grad, axis=(0, 1)))
            stacked = jnp.concatenate(
                [
                    enc_grad.astype(jnp.bfloat16).reshape(n_batch, rows_per, chunk_lat),
                    dec_grad_t.astype(jnp.bfloat16).reshape(n_batch, rows_per, chunk_lat),
                ],
                axis=2,
            )
            if c == chunks - 1:
                bias_grad = jnp.concatenate(bias_parts)
                bias_block = jnp.pad(
                    bias_grad.astype(jnp.bfloat16).reshape(n_batch, 1, bias_per),
                    ((0, 0), (0, pad_rows - 1), (0, 2 * chunk_lat - bias_per)),
                )
                stacked = jnp.concatenate([stacked, bias_block], axis=1)
            stacked = stacked.reshape(-1, 2 * chunk_lat)
            reduced.append(
                lax.psum_scatter(stacked, "batch", scatter_dimension=0, tiled=True).astype(
                    jnp.float32
                )
            )

    with jax.named_scope("grad_reduce"):
        grad_enc_weight = jnp.concatenate([r[:rows_per, :chunk_lat] for r in reduced], axis=1)
        grad_dec_weight = jnp.concatenate(
            [r[:rows_per, chunk_lat:] for r in reduced], axis=1
        ).T
        bias_share = reduced[-1][rows_per, :bias_per]
    return (grad_enc_weight, bias_share, grad_dec_weight)


def solution(mesh):
    in_specs = (
        P(("loop", "inner", "batch"), None),
        P(("loop", "inner", "batch"), None),
        P(("loop", "inner", "batch"), None, None),
        P(None, ("loop", "inner")),
        P(("loop", "inner")),
        P(("loop", "inner"), None),
        P(),
    )
    out_specs = (
        P("batch", ("loop", "inner")),
        P(("loop", "inner", "batch")),
        P(("loop", "inner"), "batch"),
    )
    return jax.shard_map(shards, mesh=mesh, in_specs=in_specs, out_specs=out_specs, check_vma=False)
```

```python
import jax
import jax.numpy as jnp
from jax import lax
from jax.sharding import PartitionSpec as P

BLK = 64
OWNER_AXES = ("loop", "inner")


def exchange(rows):
    return lax.all_to_all(rows, OWNER_AXES, split_axis=0, concat_axis=0, tiled=True)


def pick_rows(select, rows):
    return lax.dot_general(
        select, rows, (((0,), (0,)), ((), ())), preferred_element_type=jnp.float32
    ).astype(rows.dtype)


def shards(tokens, block_ids, latent_mask, enc_weight, enc_bias, dec_weight, dec_bias):
    tok_dev, model_width = tokens.shape
    pick_count = block_ids.shape[1]
    local_lat = enc_weight.shape[1]
    local_blocks = local_lat // BLK
    owners = lax.axis_size("loop") * lax.axis_size("inner")
    num_blocks = local_blocks * owners
    n_batch = lax.axis_size("batch")
    capacity = (9 * tok_dev * pick_count + 8 * num_blocks - 1) // (8 * num_blocks)
    slot_count = num_blocks * capacity
    routed = tok_dev * pick_count

    with jax.named_scope("slot_tables"):
        flat_ids = block_ids.reshape(routed)
        row_pos = jnp.arange(routed, dtype=jnp.int32)
        earlier_same = (flat_ids[:, None] == flat_ids[None, :]) & (row_pos[None, :] < row_pos[:, None])
        slot_rank = jnp.sum(earlier_same.astype(jnp.int32), axis=1)
        target = ((flat_ids // local_blocks) * capacity + slot_rank) * local_blocks + flat_ids % local_blocks
        row_to_slot = target[:, None] == jnp.arange(slot_count, dtype=jnp.int32)[None, :]
        row_to_slot = row_to_slot.astype(jnp.bfloat16)
        token_to_slot = jnp.sum(
            row_to_slot.reshape(tok_dev, pick_count, slot_count), axis=1
        ).astype(jnp.bfloat16)
        groups = slot_count // local_blocks
        token_to_group = token_to_slot.reshape(tok_dev, groups, local_blocks)

    chunks = 2
    chunk_blocks = local_blocks // chunks
    chunk_lat = chunk_blocks * BLK
    rows_per = model_width // n_batch
    bias_per = local_lat // n_batch
    pad_rows = 16

    with jax.named_scope("dispatch"):
        extra = 2 * BLK
        tokens_ext = jnp.pad(tokens, ((0, 0), (0, extra)))
        mask_rows = latent_mask.reshape(routed, BLK).astype(jnp.float32)
        send_mask = lax.dot_general(
            row_to_slot, mask_rows, (((0,), (0,)), ((), ())), preferred_element_type=jnp.float32
        ).reshape(groups, local_blocks, BLK)
        send_mask = jnp.pad(send_mask, ((0, 0), (0, 0), (model_width, extra - BLK)))
        select = [token_to_group[:, :, c * chunk_blocks:(c + 1) * chunk_blocks] for c in range(chunks)]
        payload = []
        for c in range(chunks):
            picked = lax.dot_general(
                select[c], tokens_ext, (((0,), (0,)), ((), ())), preferred_element_type=jnp.float32
            )
            picked = picked + send_mask[:, c * chunk_blocks:(c + 1) * chunk_blocks, :]
            payload.append(exchange(picked.astype(jnp.bfloat16)))
        enc_ext = jnp.pad(enc_weight, ((0, extra), (0, 0)))

    with jax.named_scope("encode_decode"):
        slot_block = jnp.arange(chunk_blocks, dtype=jnp.int32)
        col_block = jnp.arange(chunk_lat, dtype=jnp.int32) // BLK
        in_block = (slot_block[:, None] == col_block[None, :])[None]
        gates, codes, returned = [], [], []
        for c in range(chunks):
            lat = slice(c * chunk_lat, (c + 1) * chunk_lat)
            mask_c = payload[c][:, :, model_width:model_width + BLK].astype(jnp.float32)
            gate_c = jnp.where(in_block, jnp.tile(mask_c, (1, 1, chunk_blocks)), 0.0)
            preact = lax.dot_general(
                payload[c], enc_ext[:, lat], (((2,), (0,)), ((), ())),
                preferred_element_type=jnp.float32,
            )
            preact = preact + enc_bias[lat].astype(jnp.float32)[None, None, :]
            code_c = (preact * gate_c).astype(jnp.bfloat16)
            partials = lax.dot_general(
                code_c, dec_weight[lat, :], (((2,), (0,)), ((), ())),
                preferred_element_type=jnp.float32,
            ).astype(jnp.bfloat16)
            gates.append(gate_c)
            codes.append(code_c)
            returned.append(exchange(partials))
        slot_rows = payload

    with jax.named_scope("combine"):
        rebuilt = dec_bias.astype(jnp.float32)[None, :] - tokens.astype(jnp.float32)
        for c in range(chunks):
            rebuilt = rebuilt + lax.dot_general(
                select[c], returned[c], (((1, 2), (0, 1)), ((), ())),
                preferred_element_type=jnp.float32,
            )
        err_b = rebuilt.astype(jnp.bfloat16)
        error_rows = [exchange(pick_rows(select[c], err_b)) for c in range(chunks)]

    with jax.named_scope("backward"):
        reduced, bias_parts = [], []
        for c in range(chunks):
            lat = slice(c * chunk_lat, (c + 1) * chunk_lat)
            pre_grad = lax.dot_general(
                error_rows[c], dec_weight[lat, :], (((2,), (1,)), ((), ())),
                preferred_element_type=jnp.float32,
            ) * gates[c]
            pre_grad_b = pre_grad.astype(jnp.bfloat16)
            enc_grad = lax.dot_general(
                slot_rows[c], pre_grad_b, (((0, 1), (0, 1)), ((), ())),
                preferred_element_type=jnp.float32,
            )[:model_width]
            dec_grad_t = lax.dot_general(
                error_rows[c], codes[c], (((0, 1), (0, 1)), ((), ())),
                preferred_element_type=jnp.float32,
            )
            bias_parts.append(jnp.sum(pre_grad, axis=(0, 1)))
            stacked = jnp.concatenate(
                [
                    enc_grad.astype(jnp.bfloat16).reshape(n_batch, rows_per, chunk_lat),
                    dec_grad_t.astype(jnp.bfloat16).reshape(n_batch, rows_per, chunk_lat),
                ],
                axis=2,
            )
            if c == chunks - 1:
                bias_grad = jnp.concatenate(bias_parts)
                bias_block = jnp.pad(
                    bias_grad.astype(jnp.bfloat16).reshape(n_batch, 1, bias_per),
                    ((0, 0), (0, pad_rows - 1), (0, 2 * chunk_lat - bias_per)),
                )
                stacked = jnp.concatenate([stacked, bias_block], axis=1)
            stacked = stacked.reshape(-1, 2 * chunk_lat)
            reduced.append(
                lax.psum_scatter(stacked, "batch", scatter_dimension=0, tiled=True).astype(
                    jnp.float32
                )
            )

    with jax.named_scope("grad_reduce"):
        grad_enc_weight = jnp.concatenate([r[:rows_per, :chunk_lat] for r in reduced], axis=1)
        grad_dec_weight = jnp.concatenate(
            [r[:rows_per, chunk_lat:] for r in reduced], axis=1
        ).T
        bias_share = reduced[-1][rows_per, :bias_per]
    return (grad_enc_weight, bias_share, grad_dec_weight)


def solution(mesh):
    in_specs = (
        P(("loop", "inner", "batch"), None),
        P(("loop", "inner", "batch"), None),
        P(("loop", "inner", "batch"), None, None),
        P(None, ("loop", "inner")),
        P(("loop", "inner")),
        P(("loop", "inner"), None),
        P(),
    )
    out_specs = (
        P("batch", ("loop", "inner")),
        P(("loop", "inner", "batch")),
        P(("loop", "inner"), "batch"),
    )
    return jax.shard_map(shards, mesh=mesh, in_specs=in_specs, out_specs=out_specs, check_vma=False)
```

```python
import jax
import jax.numpy as jnp
from jax import lax
from jax.sharding import PartitionSpec as P

BLK = 64
OWNER_AXES = ("loop", "inner")


def exchange(rows):
    return lax.all_to_all(rows, OWNER_AXES, split_axis=0, concat_axis=0, tiled=True)


def pick_rows(select, rows):
    return lax.dot_general(
        select, rows, (((0,), (0,)), ((), ())), preferred_element_type=jnp.float32
    ).astype(rows.dtype)


def shards(tokens, block_ids, latent_mask, enc_weight, enc_bias, dec_weight, dec_bias):
    tok_dev, model_width = tokens.shape
    pick_count = block_ids.shape[1]
    local_lat = enc_weight.shape[1]
    local_blocks = local_lat // BLK
    owners = lax.axis_size("loop") * lax.axis_size("inner")
    num_blocks = local_blocks * owners
    n_batch = lax.axis_size("batch")
    capacity = (9 * tok_dev * pick_count + 8 * num_blocks - 1) // (8 * num_blocks)
    routed = tok_dev * pick_count
    main_ranks = min(capacity, (capacity * local_blocks // 8) * 8 // local_blocks)
    rank_sets = [(0, main_ranks), (main_ranks, capacity)] if main_ranks < capacity else [(0, capacity)]
    extra = 2 * BLK

    with jax.named_scope("slot_tables"):
        flat_ids = block_ids.reshape(routed)
        row_pos = jnp.arange(routed, dtype=jnp.int32)
        earlier_same = (flat_ids[:, None] == flat_ids[None, :]) & (row_pos[None, :] < row_pos[:, None])
        slot_rank = jnp.sum(earlier_same.astype(jnp.int32), axis=1)
        owner_of = flat_ids // local_blocks
        local_of = flat_ids % local_blocks
        row_to_slot, token_to_slot = [], []
        for lo, hi in rank_sets:
            per_owner = (hi - lo) * local_blocks
            target = owner_of * per_owner + (slot_rank - lo) * local_blocks + local_of
            target = jnp.where((slot_rank >= lo) & (slot_rank < hi), target, -1)
            hit = target[:, None] == jnp.arange(owners * per_owner, dtype=jnp.int32)[None, :]
            row_to_slot.append(hit.astype(jnp.bfloat16))
            token_to_slot.append(
                jnp.sum(hit.reshape(tok_dev, pick_count, -1).astype(jnp.int32), axis=1).astype(
                    jnp.bfloat16
                )
            )

    with jax.named_scope("dispatch"):
        tokens_ext = jnp.pad(tokens, ((0, 0), (0, extra)))
        mask_rows = latent_mask.reshape(routed, BLK).astype(jnp.float32)
        payload = []
        for k in range(len(rank_sets)):
            send_mask = lax.dot_general(
                row_to_slot[k], mask_rows, (((0,), (0,)), ((), ())),
                preferred_element_type=jnp.float32,
            )
            send_mask = jnp.pad(send_mask, ((0, 0), (model_width, extra - BLK)))
            picked = lax.dot_general(
                token_to_slot[k], tokens_ext, (((0,), (0,)), ((), ())),
                preferred_element_type=jnp.float32,
            )
            payload.append(exchange((picked + send_mask).astype(jnp.bfloat16)))
        enc_ext = jnp.pad(enc_weight, ((0, extra), (0, 0)))

    with jax.named_scope("encode_decode"):
        col_block = jnp.arange(local_lat, dtype=jnp.int32) // BLK
        gates, codes, returned = [], [], []
        for k in range(len(rank_sets)):
            rows = payload[k].shape[0]
            row_block = jnp.arange(rows, dtype=jnp.int32) % local_blocks
            in_block = row_block[:, None] == col_block[None, :]
            mask_k = payload[k][:, model_width:model_width + BLK].astype(jnp.float32)
            gate_k = jnp.where(in_block, jnp.tile(mask_k, (1, local_blocks)), 0.0)
            preact = jnp.dot(payload[k], enc_ext, preferred_element_type=jnp.float32)
            preact = preact + enc_bias.astype(jnp.float32)[None, :]
            code_k = (preact * gate_k).astype(jnp.bfloat16)
            partials = jnp.dot(code_k, dec_weight, preferred_element_type=jnp.float32).astype(
                jnp.bfloat16
            )
            gates.append(gate_k)
            codes.append(code_k)
            returned.append(exchange(partials))

    with jax.named_scope("combine"):
        rebuilt = dec_bias.astype(jnp.float32)[None, :] - tokens.astype(jnp.float32)
        for k in range(len(rank_sets)):
            rebuilt = rebuilt + jnp.dot(
                token_to_slot[k], returned[k], preferred_element_type=jnp.float32
            )
        err_b = rebuilt.astype(jnp.bfloat16)
        error_rows = [exchange(pick_rows(token_to_slot[k], err_b)) for k in range(len(rank_sets))]

    with jax.named_scope("backward"):
        enc_grad = dec_grad_t = bias_grad = 0.0
        for k in range(len(rank_sets)):
            pre_grad = lax.dot_general(
                error_rows[k], dec_weight, (((1,), (1,)), ((), ())),
                preferred_element_type=jnp.float32,
            ) * gates[k]
            pre_grad_b = pre_grad.astype(jnp.bfloat16)
            enc_grad = enc_grad + lax.dot_general(
                payload[k], pre_grad_b, (((0,), (0,)), ((), ())),
                preferred_element_type=jnp.float32,
            )[:model_width]
            dec_grad_t = dec_grad_t + lax.dot_general(
                error_rows[k], codes[k], (((0,), (0,)), ((), ())),
                preferred_element_type=jnp.float32,
            )
            bias_grad = bias_grad + jnp.sum(pre_grad, axis=0)

    with jax.named_scope("grad_reduce"):
        rows_per = model_width // n_batch
        bias_per = local_lat // n_batch
        pad_rows = 16
        weights = jnp.concatenate(
            [
                enc_grad.astype(jnp.bfloat16).reshape(n_batch, rows_per, local_lat),
                dec_grad_t.astype(jnp.bfloat16).reshape(n_batch, rows_per, local_lat),
            ],
            axis=2,
        )
        bias_block = jnp.pad(
            bias_grad.astype(jnp.bfloat16).reshape(n_batch, 1, bias_per),
            ((0, 0), (0, pad_rows - 1), (0, 2 * local_lat - bias_per)),
        )
        stacked = jnp.concatenate([weights, bias_block], axis=1).reshape(
            n_batch * (rows_per + pad_rows), 2 * local_lat
        )
        reduced = lax.psum_scatter(stacked, "batch", scatter_dimension=0, tiled=True).astype(
            jnp.float32
        )
        grad_enc_weight = reduced[:rows_per, :local_lat]
        grad_dec_weight = reduced[:rows_per, local_lat:].T
        bias_share = reduced[rows_per, :bias_per]
    return (grad_enc_weight, bias_share, grad_dec_weight)


def solution(mesh):
    in_specs = (
        P(("loop", "inner", "batch"), None),
        P(("loop", "inner", "batch"), None),
        P(("loop", "inner", "batch"), None, None),
        P(None, ("loop", "inner")),
        P(("loop", "inner")),
        P(("loop", "inner"), None),
        P(),
    )
    out_specs = (
        P("batch", ("loop", "inner")),
        P(("loop", "inner", "batch")),
        P(("loop", "inner"), "batch"),
    )
    return jax.shard_map(shards, mesh=mesh, in_specs=in_specs, out_specs=out_specs, check_vma=False)
```

```python
import jax
import jax.numpy as jnp
from jax import lax
from jax.sharding import PartitionSpec as P

BLK = 64
OWNER_AXES = ("loop", "inner")


def exchange(rows):
    return lax.all_to_all(rows, OWNER_AXES, split_axis=0, concat_axis=0, tiled=True)


def pick_rows(select, rows):
    return lax.dot_general(
        select, rows, (((0,), (0,)), ((), ())), preferred_element_type=jnp.float32
    ).astype(rows.dtype)


def shards(tokens, block_ids, latent_mask, enc_weight, enc_bias, dec_weight, dec_bias):
    tok_dev, model_width = tokens.shape
    pick_count = block_ids.shape[1]
    local_lat = enc_weight.shape[1]
    local_blocks = local_lat // BLK
    owners = lax.axis_size("loop") * lax.axis_size("inner")
    num_blocks = local_blocks * owners
    n_batch = lax.axis_size("batch")
    capacity = (9 * tok_dev * pick_count + 8 * num_blocks - 1) // (8 * num_blocks)
    routed = tok_dev * pick_count
    main_ranks = min(capacity, (capacity * local_blocks // 8) * 8 // local_blocks)
    rank_sets = [(0, main_ranks), (main_ranks, capacity)] if main_ranks < capacity else [(0, capacity)]
    extra = 2 * BLK

    with jax.named_scope("slot_tables"):
        flat_ids = block_ids.reshape(routed)
        row_pos = jnp.arange(routed, dtype=jnp.int32)
        earlier_same = (flat_ids[:, None] == flat_ids[None, :]) & (row_pos[None, :] < row_pos[:, None])
        slot_rank = jnp.sum(earlier_same.astype(jnp.int32), axis=1)
        owner_of = flat_ids // local_blocks
        local_of = flat_ids % local_blocks
        row_to_slot, token_to_slot = [], []
        for lo, hi in rank_sets:
            per_owner = (hi - lo) * local_blocks
            target = owner_of * per_owner + (slot_rank - lo) * local_blocks + local_of
            target = jnp.where((slot_rank >= lo) & (slot_rank < hi), target, -1)
            hit = target[:, None] == jnp.arange(owners * per_owner, dtype=jnp.int32)[None, :]
            row_to_slot.append(hit.astype(jnp.bfloat16))
            token_to_slot.append(
                jnp.sum(hit.reshape(tok_dev, pick_count, -1).astype(jnp.int32), axis=1).astype(
                    jnp.bfloat16
                )
            )

    with jax.named_scope("dispatch"):
        tokens_ext = jnp.pad(tokens, ((0, 0), (0, extra)))
        mask_rows = latent_mask.reshape(routed, BLK).astype(jnp.float32)
        payload = []
        for k in range(len(rank_sets)):
            send_mask = lax.dot_general(
                row_to_slot[k], mask_rows, (((0,), (0,)), ((), ())),
                preferred_element_type=jnp.float32,
            )
            send_mask = jnp.pad(send_mask, ((0, 0), (model_width, extra - BLK)))
            picked = lax.dot_general(
                token_to_slot[k], tokens_ext, (((0,), (0,)), ((), ())),
                preferred_element_type=jnp.float32,
            )
            payload.append(exchange((picked + send_mask).astype(jnp.bfloat16)))
        enc_ext = jnp.pad(enc_weight, ((0, extra), (0, 0)))

    with jax.named_scope("encode_decode"):
        col_block = jnp.arange(local_lat, dtype=jnp.int32) // BLK
        gates, codes, returned = [], [], []
        for k in range(len(rank_sets)):
            rows = payload[k].shape[0]
            row_block = jnp.arange(rows, dtype=jnp.int32) % local_blocks
            in_block = row_block[:, None] == col_block[None, :]
            mask_k = payload[k][:, model_width:model_width + BLK].astype(jnp.float32)
            gate_k = jnp.where(in_block, jnp.tile(mask_k, (1, local_blocks)), 0.0)
            preact = jnp.dot(payload[k], enc_ext, preferred_element_type=jnp.float32)
            preact = preact + enc_bias.astype(jnp.float32)[None, :]
            code_k = (preact * gate_k).astype(jnp.bfloat16)
            partials = jnp.dot(code_k, dec_weight, preferred_element_type=jnp.float32).astype(
                jnp.bfloat16
            )
            gates.append(gate_k)
            codes.append(code_k)
            returned.append(exchange(partials))

    with jax.named_scope("combine"):
        rebuilt = dec_bias.astype(jnp.float32)[None, :] - tokens.astype(jnp.float32)
        for k in range(len(rank_sets)):
            rebuilt = rebuilt + jnp.dot(
                token_to_slot[k], returned[k], preferred_element_type=jnp.float32
            )
        err_b = rebuilt.astype(jnp.bfloat16)
        error_rows = []
        for k in range(len(rank_sets)):
            send_err = pick_rows(token_to_slot[k], err_b)
            if error_rows:
                send_err = send_err + 0 * error_rows[0][:1, :1]
            error_rows.append(exchange(send_err))

    with jax.named_scope("backward"):
        enc_grad = dec_grad_t = bias_grad = 0.0
        for k in range(len(rank_sets)):
            pre_grad = lax.dot_general(
                error_rows[k], dec_weight, (((1,), (1,)), ((), ())),
                preferred_element_type=jnp.float32,
            ) * gates[k]
            pre_grad_b = pre_grad.astype(jnp.bfloat16)
            enc_grad = enc_grad + lax.dot_general(
                payload[k], pre_grad_b, (((0,), (0,)), ((), ())),
                preferred_element_type=jnp.float32,
            )[:model_width]
            dec_grad_t = dec_grad_t + lax.dot_general(
                error_rows[k], codes[k], (((0,), (0,)), ((), ())),
                preferred_element_type=jnp.float32,
            )
            bias_grad = bias_grad + jnp.sum(pre_grad, axis=0)
            if k == 0:
                enc_grad, dec_grad_t, bias_grad = lax.optimization_barrier(
                    (enc_grad, dec_grad_t, bias_grad)
                )

    with jax.named_scope("grad_reduce"):
        rows_per = model_width // n_batch
        bias_per = local_lat // n_batch
        pad_rows = 16
        weights = jnp.concatenate(
            [
                enc_grad.astype(jnp.bfloat16).reshape(n_batch, rows_per, local_lat),
                dec_grad_t.astype(jnp.bfloat16).reshape(n_batch, rows_per, local_lat),
            ],
            axis=2,
        )
        bias_block = jnp.pad(
            bias_grad.astype(jnp.bfloat16).reshape(n_batch, 1, bias_per),
            ((0, 0), (0, pad_rows - 1), (0, 2 * local_lat - bias_per)),
        )
        stacked = jnp.concatenate([weights, bias_block], axis=1).reshape(
            n_batch * (rows_per + pad_rows), 2 * local_lat
        )
        reduced = lax.psum_scatter(stacked, "batch", scatter_dimension=0, tiled=True).astype(
            jnp.float32
        )
        grad_enc_weight = reduced[:rows_per, :local_lat]
        grad_dec_weight = reduced[:rows_per, local_lat:].T
        bias_share = reduced[rows_per, :bias_per]
    return (grad_enc_weight, bias_share, grad_dec_weight)


def solution(mesh):
    in_specs = (
        P(("loop", "inner", "batch"), None),
        P(("loop", "inner", "batch"), None),
        P(("loop", "inner", "batch"), None, None),
        P(None, ("loop", "inner")),
        P(("loop", "inner")),
        P(("loop", "inner"), None),
        P(),
    )
    out_specs = (
        P("batch", ("loop", "inner")),
        P(("loop", "inner", "batch")),
        P(("loop", "inner"), "batch"),
    )
    return jax.shard_map(shards, mesh=mesh, in_specs=in_specs, out_specs=out_specs, check_vma=False)
```

```python
import jax
import jax.numpy as jnp
from jax import lax
from jax.sharding import PartitionSpec as P

BLK = 64
OWNER_AXES = ("loop", "inner")


def exchange(rows):
    return lax.all_to_all(rows, OWNER_AXES, split_axis=0, concat_axis=0, tiled=True)


def pick_rows(select, rows):
    return lax.dot_general(
        select, rows, (((0,), (0,)), ((), ())), preferred_element_type=jnp.float32
    ).astype(rows.dtype)


def shards(tokens, block_ids, latent_mask, enc_weight, enc_bias, dec_weight, dec_bias):
    tok_dev, model_width = tokens.shape
    pick_count = block_ids.shape[1]
    local_lat = enc_weight.shape[1]
    local_blocks = local_lat // BLK
    owners = lax.axis_size("loop") * lax.axis_size("inner")
    num_blocks = local_blocks * owners
    n_batch = lax.axis_size("batch")
    capacity = (9 * tok_dev * pick_count + 8 * num_blocks - 1) // (8 * num_blocks)
    routed = tok_dev * pick_count
    main_ranks = min(capacity, (capacity * local_blocks // 8) * 8 // local_blocks)
    rank_sets = [(0, main_ranks), (main_ranks, capacity)] if main_ranks < capacity else [(0, capacity)]
    extra = 2 * BLK

    with jax.named_scope("slot_tables"):
        flat_ids = block_ids.reshape(routed)
        row_pos = jnp.arange(routed, dtype=jnp.int32)
        earlier_same = (flat_ids[:, None] == flat_ids[None, :]) & (row_pos[None, :] < row_pos[:, None])
        slot_rank = jnp.sum(earlier_same.astype(jnp.int32), axis=1)
        owner_of = flat_ids // local_blocks
        local_of = flat_ids % local_blocks
        row_to_slot, token_to_slot = [], []
        for lo, hi in rank_sets:
            per_owner = (hi - lo) * local_blocks
            target = owner_of * per_owner + (slot_rank - lo) * local_blocks + local_of
            target = jnp.where((slot_rank >= lo) & (slot_rank < hi), target, -1)
            hit = target[:, None] == jnp.arange(owners * per_owner, dtype=jnp.int32)[None, :]
            row_to_slot.append(hit.astype(jnp.bfloat16))
            token_to_slot.append(
                jnp.sum(hit.reshape(tok_dev, pick_count, -1).astype(jnp.int32), axis=1).astype(
                    jnp.bfloat16
                )
            )

    with jax.named_scope("dispatch"):
        tokens_ext = jnp.pad(tokens, ((0, 0), (0, extra)))
        mask_rows = latent_mask.reshape(routed, BLK).astype(jnp.float32)
        payload = []
        for k in range(len(rank_sets)):
            send_mask = lax.dot_general(
                row_to_slot[k], mask_rows, (((0,), (0,)), ((), ())),
                preferred_element_type=jnp.float32,
            )
            send_mask = jnp.pad(send_mask, ((0, 0), (model_width, extra - BLK)))
            picked = lax.dot_general(
                token_to_slot[k], tokens_ext, (((0,), (0,)), ((), ())),
                preferred_element_type=jnp.float32,
            )
            payload.append(exchange((picked + send_mask).astype(jnp.bfloat16)))
        enc_ext = jnp.pad(enc_weight, ((0, extra), (0, 0)))

    with jax.named_scope("encode_decode"):
        col_block = jnp.arange(local_lat, dtype=jnp.int32) // BLK
        gates, codes, returned = [], [], []
        for k in range(len(rank_sets)):
            rows = payload[k].shape[0]
            row_block = jnp.arange(rows, dtype=jnp.int32) % local_blocks
            in_block = row_block[:, None] == col_block[None, :]
            mask_k = payload[k][:, model_width:model_width + BLK].astype(jnp.float32)
            gate_k = jnp.where(in_block, jnp.tile(mask_k, (1, local_blocks)), 0.0)
            preact = jnp.dot(payload[k], enc_ext, preferred_element_type=jnp.float32)
            preact = preact + enc_bias.astype(jnp.float32)[None, :]
            code_k = (preact * gate_k).astype(jnp.bfloat16)
            partials = jnp.dot(code_k, dec_weight, preferred_element_type=jnp.float32).astype(
                jnp.bfloat16
            )
            gates.append(gate_k)
            codes.append(code_k)
            returned.append(exchange(partials))

    with jax.named_scope("combine"):
        rebuilt = dec_bias.astype(jnp.float32)[None, :] - tokens.astype(jnp.float32)
        for k in range(len(rank_sets)):
            rebuilt = rebuilt + jnp.dot(
                token_to_slot[k], returned[k], preferred_element_type=jnp.float32
            )
        err_b = rebuilt.astype(jnp.bfloat16)
        error_rows = [exchange(pick_rows(token_to_slot[k], err_b)) for k in range(len(rank_sets))]

    with jax.named_scope("backward"):
        enc_parts, dec_parts, bias_grad = [], [], 0.0
        for k in range(len(rank_sets)):
            pre_grad = lax.dot_general(
                error_rows[k], dec_weight, (((1,), (1,)), ((), ())),
                preferred_element_type=jnp.float32,
            ) * gates[k]
            pre_grad_b = pre_grad.astype(jnp.bfloat16)
            enc_parts.append(lax.dot_general(
                payload[k], pre_grad_b, (((0,), (0,)), ((), ())),
                preferred_element_type=jnp.float32,
            )[:model_width])
            dec_parts.append(lax.dot_general(
                error_rows[k], codes[k], (((0,), (0,)), ((), ())),
                preferred_element_type=jnp.float32,
            ))
            bias_grad = bias_grad + jnp.sum(pre_grad, axis=0)
        enc_grad, dec_grad_t = enc_parts[0], dec_parts[0]
        for k in range(1, len(rank_sets)):
            enc_grad = enc_grad + enc_parts[k].astype(jnp.bfloat16).astype(jnp.float32)
            dec_grad_t = dec_grad_t + dec_parts[k].astype(jnp.bfloat16).astype(jnp.float32)
        enc_grad = enc_grad.astype(jnp.bfloat16)
        dec_grad_t = dec_grad_t.astype(jnp.bfloat16)

    with jax.named_scope("grad_reduce"):
        rows_per = model_width // n_batch
        bias_per = local_lat // n_batch
        pad_rows = 16
        weights = jnp.concatenate(
            [
                enc_grad.reshape(n_batch, rows_per, local_lat),
                dec_grad_t.reshape(n_batch, rows_per, local_lat),
            ],
            axis=2,
        )
        bias_block = jnp.pad(
            bias_grad.astype(jnp.bfloat16).reshape(n_batch, 1, bias_per),
            ((0, 0), (0, pad_rows - 1), (0, 2 * local_lat - bias_per)),
        )
        stacked = jnp.concatenate([weights, bias_block], axis=1).reshape(
            n_batch * (rows_per + pad_rows), 2 * local_lat
        )
        reduced = lax.psum_scatter(stacked, "batch", scatter_dimension=0, tiled=True).astype(
            jnp.float32
        )
        grad_enc_weight = reduced[:rows_per, :local_lat]
        grad_dec_weight = reduced[:rows_per, local_lat:].T
        bias_share = reduced[rows_per, :bias_per]
    return (grad_enc_weight, bias_share, grad_dec_weight)


def solution(mesh):
    in_specs = (
        P(("loop", "inner", "batch"), None),
        P(("loop", "inner", "batch"), None),
        P(("loop", "inner", "batch"), None, None),
        P(None, ("loop", "inner")),
        P(("loop", "inner")),
        P(("loop", "inner"), None),
        P(),
    )
    out_specs = (
        P("batch", ("loop", "inner")),
        P(("loop", "inner", "batch")),
        P(("loop", "inner"), "batch"),
    )
    return jax.shard_map(shards, mesh=mesh, in_specs=in_specs, out_specs=out_specs, check_vma=False)
```

```python
import jax
import jax.numpy as jnp
from jax import lax
from jax.sharding import PartitionSpec as P

BLK = 64
OWNER_AXES = ("loop", "inner")


def exchange(rows):
    return lax.all_to_all(rows, OWNER_AXES, split_axis=0, concat_axis=0, tiled=True)


def pick_rows(select, rows):
    return lax.dot_general(
        select, rows, (((0,), (0,)), ((), ())), preferred_element_type=jnp.float32
    ).astype(rows.dtype)


def shards(tokens, block_ids, latent_mask, enc_weight, enc_bias, dec_weight, dec_bias):
    tok_dev, model_width = tokens.shape
    pick_count = block_ids.shape[1]
    local_lat = enc_weight.shape[1]
    local_blocks = local_lat // BLK
    owners = lax.axis_size("loop") * lax.axis_size("inner")
    num_blocks = local_blocks * owners
    n_batch = lax.axis_size("batch")
    capacity = (9 * tok_dev * pick_count + 8 * num_blocks - 1) // (8 * num_blocks)
    routed = tok_dev * pick_count
    main_ranks = min(capacity, (capacity * local_blocks // 8) * 8 // local_blocks)
    rank_sets = [(0, main_ranks), (main_ranks, capacity)] if main_ranks < capacity else [(0, capacity)]
    extra = 2 * BLK

    with jax.named_scope("slot_tables"):
        flat_ids = block_ids.reshape(routed)
        row_pos = jnp.arange(routed, dtype=jnp.int32)
        earlier_same = (flat_ids[:, None] == flat_ids[None, :]) & (row_pos[None, :] < row_pos[:, None])
        slot_rank = jnp.sum(earlier_same.astype(jnp.int32), axis=1)
        owner_of = flat_ids // local_blocks
        local_of = flat_ids % local_blocks
        row_to_slot, token_to_slot = [], []
        for lo, hi in rank_sets:
            per_owner = (hi - lo) * local_blocks
            target = owner_of * per_owner + (slot_rank - lo) * local_blocks + local_of
            target = jnp.where((slot_rank >= lo) & (slot_rank < hi), target, -1)
            hit = target[:, None] == jnp.arange(owners * per_owner, dtype=jnp.int32)[None, :]
            row_to_slot.append(hit.astype(jnp.bfloat16))
            token_to_slot.append(
                jnp.sum(hit.reshape(tok_dev, pick_count, -1).astype(jnp.int32), axis=1).astype(
                    jnp.bfloat16
                )
            )

    with jax.named_scope("dispatch"):
        tokens_ext = jnp.pad(tokens, ((0, 0), (0, extra)))
        mask_rows = latent_mask.reshape(routed, BLK).astype(jnp.float32)
        payload = []
        for k in range(len(rank_sets)):
            send_mask = lax.dot_general(
                row_to_slot[k], mask_rows, (((0,), (0,)), ((), ())),
                preferred_element_type=jnp.float32,
            )
            send_mask = jnp.pad(send_mask, ((0, 0), (model_width, extra - BLK)))
            picked = lax.dot_general(
                token_to_slot[k], tokens_ext, (((0,), (0,)), ((), ())),
                preferred_element_type=jnp.float32,
            )
            payload.append(exchange((picked + send_mask).astype(jnp.bfloat16)))
        enc_ext = jnp.pad(enc_weight, ((0, extra), (0, 0)))

    with jax.named_scope("encode_decode"):
        col_block = jnp.arange(local_lat, dtype=jnp.int32) // BLK
        gates, codes, returned = [], [], []
        for k in range(len(rank_sets)):
            rows = payload[k].shape[0]
            row_block = jnp.arange(rows, dtype=jnp.int32) % local_blocks
            in_block = row_block[:, None] == col_block[None, :]
            mask_k = payload[k][:, model_width:model_width + BLK].astype(jnp.float32)
            gate_k = jnp.where(in_block, jnp.tile(mask_k, (1, local_blocks)), 0.0)
            preact = jnp.dot(payload[k], enc_ext, preferred_element_type=jnp.float32)
            preact = preact + enc_bias.astype(jnp.float32)[None, :]
            code_k = (preact * gate_k).astype(jnp.bfloat16)
            partials = jnp.dot(code_k, dec_weight, preferred_element_type=jnp.float32).astype(
                jnp.bfloat16
            )
            gates.append(gate_k)
            codes.append(code_k)
            returned.append(exchange(partials))

    with jax.named_scope("combine"):
        rebuilt = dec_bias.astype(jnp.float32)[None, :] - tokens.astype(jnp.float32)
        for k in range(len(rank_sets)):
            rebuilt = rebuilt + jnp.dot(
                token_to_slot[k], returned[k], preferred_element_type=jnp.float32
            )
        err_b = rebuilt.astype(jnp.bfloat16)
        error_rows = []
        for k in range(len(rank_sets)):
            send_err = pick_rows(token_to_slot[k], err_b)
            if error_rows:
                send_err = send_err + 0 * error_rows[0][:1, :1]
            error_rows.append(exchange(send_err))

    with jax.named_scope("backward"):
        enc_grad = dec_grad_t = bias_grad = 0.0
        for k in range(len(rank_sets)):
            pre_grad = lax.dot_general(
                error_rows[k], dec_weight, (((1,), (1,)), ((), ())),
                preferred_element_type=jnp.float32,
            ) * gates[k]
            pre_grad_b = pre_grad.astype(jnp.bfloat16)
            enc_grad = enc_grad + lax.dot_general(
                payload[k], pre_grad_b, (((0,), (0,)), ((), ())),
                preferred_element_type=jnp.float32,
            )[:model_width]
            dec_grad_t = dec_grad_t + lax.dot_general(
                error_rows[k], codes[k], (((0,), (0,)), ((), ())),
                preferred_element_type=jnp.float32,
            )
            bias_grad = bias_grad + jnp.sum(pre_grad, axis=0)
            if k == 0:
                enc_b, dec_b, bias_grad = lax.optimization_barrier(
                    (enc_grad.astype(jnp.bfloat16), dec_grad_t.astype(jnp.bfloat16), bias_grad)
                )
                enc_grad, dec_grad_t = enc_b.astype(jnp.float32), dec_b.astype(jnp.float32)

    with jax.named_scope("grad_reduce"):
        rows_per = model_width // n_batch
        bias_per = local_lat // n_batch
        pad_rows = 16
        weights = jnp.concatenate(
            [
                enc_grad.astype(jnp.bfloat16).reshape(n_batch, rows_per, local_lat),
                dec_grad_t.astype(jnp.bfloat16).reshape(n_batch, rows_per, local_lat),
            ],
            axis=2,
        )
        bias_block = jnp.pad(
            bias_grad.astype(jnp.bfloat16).reshape(n_batch, 1, bias_per),
            ((0, 0), (0, pad_rows - 1), (0, 2 * local_lat - bias_per)),
        )
        stacked = jnp.concatenate([weights, bias_block], axis=1).reshape(
            n_batch * (rows_per + pad_rows), 2 * local_lat
        )
        reduced = lax.psum_scatter(stacked, "batch", scatter_dimension=0, tiled=True).astype(
            jnp.float32
        )
        grad_enc_weight = reduced[:rows_per, :local_lat]
        grad_dec_weight = reduced[:rows_per, local_lat:].T
        bias_share = reduced[rows_per, :bias_per]
    return (grad_enc_weight, bias_share, grad_dec_weight)


def solution(mesh):
    in_specs = (
        P(("loop", "inner", "batch"), None),
        P(("loop", "inner", "batch"), None),
        P(("loop", "inner", "batch"), None, None),
        P(None, ("loop", "inner")),
        P(("loop", "inner")),
        P(("loop", "inner"), None),
        P(),
    )
    out_specs = (
        P("batch", ("loop", "inner")),
        P(("loop", "inner", "batch")),
        P(("loop", "inner"), "batch"),
    )
    return jax.shard_map(shards, mesh=mesh, in_specs=in_specs, out_specs=out_specs, check_vma=False)
```

```python
import jax
import jax.numpy as jnp
from jax import lax
from jax.sharding import PartitionSpec as P

BLK = 64
OWNER_AXES = ("loop", "inner")


def exchange(rows):
    return lax.all_to_all(rows, OWNER_AXES, split_axis=0, concat_axis=0, tiled=True)


def pick_rows(select, rows):
    return lax.dot_general(
        select, rows, (((0,), (0,)), ((), ())), preferred_element_type=jnp.float32
    ).astype(rows.dtype)


def shards(tokens, block_ids, latent_mask, enc_weight, enc_bias, dec_weight, dec_bias):
    tok_dev, model_width = tokens.shape
    pick_count = block_ids.shape[1]
    local_lat = enc_weight.shape[1]
    local_blocks = local_lat // BLK
    owners = lax.axis_size("loop") * lax.axis_size("inner")
    num_blocks = local_blocks * owners
    n_batch = lax.axis_size("batch")
    capacity = (9 * tok_dev * pick_count + 8 * num_blocks - 1) // (8 * num_blocks)
    routed = tok_dev * pick_count
    main_ranks = min(capacity, (capacity * local_blocks // 8) * 8 // local_blocks)
    rank_sets = [(0, main_ranks), (main_ranks, capacity)] if main_ranks < capacity else [(0, capacity)]
    extra = 2 * BLK

    with jax.named_scope("slot_tables"):
        flat_ids = block_ids.reshape(routed)
        row_pos = jnp.arange(routed, dtype=jnp.int32)
        earlier_same = (flat_ids[:, None] == flat_ids[None, :]) & (row_pos[None, :] < row_pos[:, None])
        slot_rank = jnp.sum(earlier_same.astype(jnp.int32), axis=1)
        owner_of = flat_ids // local_blocks
        local_of = flat_ids % local_blocks
        row_to_slot, token_to_slot = [], []
        for lo, hi in rank_sets:
            per_owner = (hi - lo) * local_blocks
            target = owner_of * per_owner + (slot_rank - lo) * local_blocks + local_of
            target = jnp.where((slot_rank >= lo) & (slot_rank < hi), target, -1)
            hit = target[:, None] == jnp.arange(owners * per_owner, dtype=jnp.int32)[None, :]
            row_to_slot.append(hit.astype(jnp.bfloat16))
            token_to_slot.append(
                jnp.sum(hit.reshape(tok_dev, pick_count, -1).astype(jnp.int32), axis=1).astype(
                    jnp.bfloat16
                )
            )

    with jax.named_scope("dispatch"):
        tokens_ext = jnp.pad(tokens, ((0, 0), (0, extra)))
        mask_rows = latent_mask.reshape(routed, BLK).astype(jnp.float32)
        payload = []
        for k in range(len(rank_sets)):
            send_mask = lax.dot_general(
                row_to_slot[k], mask_rows, (((0,), (0,)), ((), ())),
                preferred_element_type=jnp.float32,
            )
            send_mask = jnp.pad(send_mask, ((0, 0), (model_width, extra - BLK)))
            picked = lax.dot_general(
                token_to_slot[k], tokens_ext, (((0,), (0,)), ((), ())),
                preferred_element_type=jnp.float32,
            )
            payload.append(exchange((picked + send_mask).astype(jnp.bfloat16)))
        enc_ext = jnp.pad(enc_weight, ((0, extra), (0, 0)))

    with jax.named_scope("encode_decode"):
        col_block = jnp.arange(local_lat, dtype=jnp.int32) // BLK
        gates, codes, returned = [], [], []
        for k in range(len(rank_sets)):
            rows = payload[k].shape[0]
            row_block = jnp.arange(rows, dtype=jnp.int32) % local_blocks
            in_block = row_block[:, None] == col_block[None, :]
            mask_k = payload[k][:, model_width:model_width + BLK].astype(jnp.float32)
            gate_k = jnp.where(in_block, jnp.tile(mask_k, (1, local_blocks)), 0.0)
            preact = jnp.dot(payload[k], enc_ext, preferred_element_type=jnp.float32)
            preact = preact + enc_bias.astype(jnp.float32)[None, :]
            code_k = (preact * gate_k).astype(jnp.bfloat16)
            partials = jnp.dot(code_k, dec_weight, preferred_element_type=jnp.float32).astype(
                jnp.bfloat16
            )
            gates.append(gate_k)
            codes.append(code_k)
            returned.append(exchange(partials))

    with jax.named_scope("combine"):
        rebuilt = dec_bias.astype(jnp.float32)[None, :] - tokens.astype(jnp.float32)
        for k in range(len(rank_sets)):
            rebuilt = rebuilt + jnp.dot(
                token_to_slot[k], returned[k], preferred_element_type=jnp.float32
            )
        err_b = rebuilt.astype(jnp.bfloat16)
        send_err = [pick_rows(token_to_slot[k], err_b) for k in range(len(rank_sets))]
        error_rows = [exchange(send_err[0])]
        held, rest = lax.optimization_barrier((error_rows[0], send_err[1:]))
        error_rows[0] = held
        error_rows += [exchange(r) for r in rest]

    with jax.named_scope("backward"):
        enc_grad = dec_grad_t = bias_grad = 0.0
        for k in range(len(rank_sets)):
            pre_grad = lax.dot_general(
                error_rows[k], dec_weight, (((1,), (1,)), ((), ())),
                preferred_element_type=jnp.float32,
            ) * gates[k]
            pre_grad_b = pre_grad.astype(jnp.bfloat16)
            enc_grad = enc_grad + lax.dot_general(
                payload[k], pre_grad_b, (((0,), (0,)), ((), ())),
                preferred_element_type=jnp.float32,
            )[:model_width]
            dec_grad_t = dec_grad_t + lax.dot_general(
                error_rows[k], codes[k], (((0,), (0,)), ((), ())),
                preferred_element_type=jnp.float32,
            )
            bias_grad = bias_grad + jnp.sum(pre_grad, axis=0)
            if k == 0:
                enc_b, dec_b, bias_grad = lax.optimization_barrier(
                    (enc_grad.astype(jnp.bfloat16), dec_grad_t.astype(jnp.bfloat16), bias_grad)
                )
                enc_grad, dec_grad_t = enc_b.astype(jnp.float32), dec_b.astype(jnp.float32)

    with jax.named_scope("grad_reduce"):
        rows_per = model_width // n_batch
        bias_per = local_lat // n_batch
        pad_rows = 16
        weights = jnp.concatenate(
            [
                enc_grad.astype(jnp.bfloat16).reshape(n_batch, rows_per, local_lat),
                dec_grad_t.astype(jnp.bfloat16).reshape(n_batch, rows_per, local_lat),
            ],
            axis=2,
        )
        bias_block = jnp.pad(
            bias_grad.astype(jnp.bfloat16).reshape(n_batch, 1, bias_per),
            ((0, 0), (0, pad_rows - 1), (0, 2 * local_lat - bias_per)),
        )
        stacked = jnp.concatenate([weights, bias_block], axis=1).reshape(
            n_batch * (rows_per + pad_rows), 2 * local_lat
        )
        reduced = lax.psum_scatter(stacked, "batch", scatter_dimension=0, tiled=True).astype(
            jnp.float32
        )
        grad_enc_weight = reduced[:rows_per, :local_lat]
        grad_dec_weight = reduced[:rows_per, local_lat:].T
        bias_share = reduced[rows_per, :bias_per]
    return (grad_enc_weight, bias_share, grad_dec_weight)


def solution(mesh):
    in_specs = (
        P(("loop", "inner", "batch"), None),
        P(("loop", "inner", "batch"), None),
        P(("loop", "inner", "batch"), None, None),
        P(None, ("loop", "inner")),
        P(("loop", "inner")),
        P(("loop", "inner"), None),
        P(),
    )
    out_specs = (
        P("batch", ("loop", "inner")),
        P(("loop", "inner", "batch")),
        P(("loop", "inner"), "batch"),
    )
    return jax.shard_map(shards, mesh=mesh, in_specs=in_specs, out_specs=out_specs, check_vma=False)
```

```python
import jax
import jax.numpy as jnp
from jax import lax
from jax.sharding import PartitionSpec as P

BLK = 64
OWNER_AXES = ("loop", "inner")


def exchange(rows):
    return lax.all_to_all(rows, OWNER_AXES, split_axis=0, concat_axis=0, tiled=True)


def pick_rows(select, rows):
    return lax.dot_general(
        select, rows, (((0,), (0,)), ((), ())), preferred_element_type=jnp.float32
    ).astype(rows.dtype)


def shards(tokens, block_ids, latent_mask, enc_weight, enc_bias, dec_weight, dec_bias):
    tok_dev, model_width = tokens.shape
    pick_count = block_ids.shape[1]
    local_lat = enc_weight.shape[1]
    local_blocks = local_lat // BLK
    owners = lax.axis_size("loop") * lax.axis_size("inner")
    num_blocks = local_blocks * owners
    n_batch = lax.axis_size("batch")
    capacity = (9 * tok_dev * pick_count + 8 * num_blocks - 1) // (8 * num_blocks)
    routed = tok_dev * pick_count
    main_ranks = min(capacity, (capacity * local_blocks // 8) * 8 // local_blocks)
    rank_sets = [(0, main_ranks), (main_ranks, capacity)] if main_ranks < capacity else [(0, capacity)]
    extra = 2 * BLK

    with jax.named_scope("slot_tables"):
        flat_ids = block_ids.reshape(routed)
        row_pos = jnp.arange(routed, dtype=jnp.int32)
        earlier_same = (flat_ids[:, None] == flat_ids[None, :]) & (row_pos[None, :] < row_pos[:, None])
        slot_rank = jnp.sum(earlier_same.astype(jnp.int32), axis=1)
        owner_of = flat_ids // local_blocks
        local_of = flat_ids % local_blocks
        row_to_slot, token_to_slot = [], []
        for lo, hi in rank_sets:
            per_owner = (hi - lo) * local_blocks
            target = owner_of * per_owner + (slot_rank - lo) * local_blocks + local_of
            target = jnp.where((slot_rank >= lo) & (slot_rank < hi), target, -1)
            hit = target[:, None] == jnp.arange(owners * per_owner, dtype=jnp.int32)[None, :]
            row_to_slot.append(hit.astype(jnp.bfloat16))
            token_to_slot.append(
                jnp.sum(hit.reshape(tok_dev, pick_count, -1).astype(jnp.int32), axis=1).astype(
                    jnp.bfloat16
                )
            )

    with jax.named_scope("dispatch"):
        tokens_ext = jnp.pad(tokens, ((0, 0), (0, extra)))
        mask_rows = latent_mask.reshape(routed, BLK).astype(jnp.float32)
        payload = []
        for k in range(len(rank_sets)):
            send_mask = lax.dot_general(
                row_to_slot[k], mask_rows, (((0,), (0,)), ((), ())),
                preferred_element_type=jnp.float32,
            )
            send_mask = jnp.pad(send_mask, ((0, 0), (model_width, extra - BLK)))
            picked = lax.dot_general(
                token_to_slot[k], tokens_ext, (((0,), (0,)), ((), ())),
                preferred_element_type=jnp.float32,
            )
            payload.append(exchange((picked + send_mask).astype(jnp.bfloat16)))
        enc_ext = jnp.pad(enc_weight, ((0, extra), (0, 0)))

    with jax.named_scope("encode_decode"):
        col_block = jnp.arange(local_lat, dtype=jnp.int32) // BLK
        gates, codes, returned = [], [], []
        for k in range(len(rank_sets)):
            rows = payload[k].shape[0]
            row_block = jnp.arange(rows, dtype=jnp.int32) % local_blocks
            in_block = row_block[:, None] == col_block[None, :]
            mask_k = payload[k][:, model_width:model_width + BLK].astype(jnp.float32)
            gate_k = jnp.where(in_block, jnp.tile(mask_k, (1, local_blocks)), 0.0)
            preact = jnp.dot(payload[k], enc_ext, preferred_element_type=jnp.float32)
            preact = preact + enc_bias.astype(jnp.float32)[None, :]
            code_k = (preact * gate_k).astype(jnp.bfloat16)
            partials = jnp.dot(code_k, dec_weight, preferred_element_type=jnp.float32).astype(
                jnp.bfloat16
            )
            gates.append(gate_k)
            codes.append(code_k)
            returned.append(exchange(partials))

    with jax.named_scope("combine"):
        rebuilt = dec_bias.astype(jnp.float32)[None, :] - tokens.astype(jnp.float32)
        for k in range(len(rank_sets)):
            rebuilt = rebuilt + jnp.dot(
                token_to_slot[k], returned[k], preferred_element_type=jnp.float32
            )
        err_b = rebuilt.astype(jnp.bfloat16)
        error_rows = []
        for k in range(len(rank_sets)):
            send_err = pick_rows(token_to_slot[k], err_b)
            if error_rows:
                send_err = send_err + 0 * error_rows[0][:1, :1]
            error_rows.append(exchange(send_err))

    with jax.named_scope("backward"):
        enc_grad = dec_grad_t = bias_grad = 0.0
        for k in range(len(rank_sets)):
            pre_grad = lax.dot_general(
                error_rows[k], dec_weight, (((1,), (1,)), ((), ())),
                preferred_element_type=jnp.float32,
            ) * gates[k]
            pre_grad_b = pre_grad.astype(jnp.bfloat16)
            enc_grad = enc_grad + lax.dot_general(
                payload[k], pre_grad_b, (((0,), (0,)), ((), ())),
                preferred_element_type=jnp.float32,
            )[:model_width]
            dec_grad_t = dec_grad_t + lax.dot_general(
                error_rows[k], codes[k], (((0,), (0,)), ((), ())),
                preferred_element_type=jnp.float32,
            )
            bias_grad = bias_grad + jnp.sum(pre_grad, axis=0)
            if k == 0:
                enc_b, dec_b, bias_grad = lax.optimization_barrier(
                    (enc_grad.astype(jnp.bfloat16), dec_grad_t.astype(jnp.bfloat16), bias_grad)
                )
                enc_grad, dec_grad_t = enc_b.astype(jnp.float32), dec_b.astype(jnp.float32)

    with jax.named_scope("grad_reduce"):
        rows_per = model_width // n_batch
        bias_per = local_lat // n_batch
        pad_rows = 8
        weights = jnp.concatenate(
            [
                enc_grad.astype(jnp.bfloat16).reshape(n_batch, rows_per, local_lat),
                dec_grad_t.astype(jnp.bfloat16).reshape(n_batch, rows_per, local_lat),
            ],
            axis=2,
        )
        bias_block = jnp.pad(
            bias_grad.astype(jnp.bfloat16).reshape(n_batch, 1, bias_per),
            ((0, 0), (0, pad_rows - 1), (0, 2 * local_lat - bias_per)),
        )
        stacked = jnp.concatenate([weights, bias_block], axis=1).reshape(
            n_batch * (rows_per + pad_rows), 2 * local_lat
        )
        reduced = lax.psum_scatter(stacked, "batch", scatter_dimension=0, tiled=True).astype(
            jnp.float32
        )
        grad_enc_weight = reduced[:rows_per, :local_lat]
        grad_dec_weight = reduced[:rows_per, local_lat:].T
        bias_share = reduced[rows_per, :bias_per]
    return (grad_enc_weight, bias_share, grad_dec_weight)


def solution(mesh):
    in_specs = (
        P(("loop", "inner", "batch"), None),
        P(("loop", "inner", "batch"), None),
        P(("loop", "inner", "batch"), None, None),
        P(None, ("loop", "inner")),
        P(("loop", "inner")),
        P(("loop", "inner"), None),
        P(),
    )
    out_specs = (
        P("batch", ("loop", "inner")),
        P(("loop", "inner", "batch")),
        P(("loop", "inner"), "batch"),
    )
    return jax.shard_map(shards, mesh=mesh, in_specs=in_specs, out_specs=out_specs, check_vma=False)
```

```python
import jax
import jax.numpy as jnp
from jax import lax
from jax.sharding import PartitionSpec as P

BLK = 64
OWNER_AXES = ("loop", "inner")


def exchange(rows):
    return lax.all_to_all(rows, OWNER_AXES, split_axis=0, concat_axis=0, tiled=True)


def pick_rows(select, rows):
    return lax.dot_general(
        select, rows, (((0,), (0,)), ((), ())), preferred_element_type=jnp.float32
    ).astype(rows.dtype)


def shards(tokens, block_ids, latent_mask, enc_weight, enc_bias, dec_weight, dec_bias):
    tok_dev, model_width = tokens.shape
    pick_count = block_ids.shape[1]
    local_lat = enc_weight.shape[1]
    local_blocks = local_lat // BLK
    owners = lax.axis_size("loop") * lax.axis_size("inner")
    num_blocks = local_blocks * owners
    n_batch = lax.axis_size("batch")
    capacity = (9 * tok_dev * pick_count + 8 * num_blocks - 1) // (8 * num_blocks)
    routed = tok_dev * pick_count
    main_ranks = min(capacity, (capacity * local_blocks // 8) * 8 // local_blocks)
    rank_sets = [(0, main_ranks), (main_ranks, capacity)] if main_ranks < capacity else [(0, capacity)]
    extra = 2 * BLK

    with jax.named_scope("slot_tables"):
        flat_ids = block_ids.reshape(routed)
        row_pos = jnp.arange(routed, dtype=jnp.int32)
        earlier_same = (flat_ids[:, None] == flat_ids[None, :]) & (row_pos[None, :] < row_pos[:, None])
        slot_rank = jnp.sum(earlier_same.astype(jnp.int32), axis=1)
        owner_of = flat_ids // local_blocks
        local_of = flat_ids % local_blocks
        row_to_slot, token_to_slot = [], []
        for lo, hi in rank_sets:
            per_owner = (hi - lo) * local_blocks
            target = owner_of * per_owner + (slot_rank - lo) * local_blocks + local_of
            target = jnp.where((slot_rank >= lo) & (slot_rank < hi), target, -1)
            hit = target[:, None] == jnp.arange(owners * per_owner, dtype=jnp.int32)[None, :]
            row_to_slot.append(hit.astype(jnp.bfloat16))
            token_to_slot.append(
                jnp.sum(hit.reshape(tok_dev, pick_count, -1).astype(jnp.int32), axis=1).astype(
                    jnp.bfloat16
                )
            )

    with jax.named_scope("dispatch"):
        tokens_ext = jnp.pad(tokens, ((0, 0), (0, extra)))
        mask_rows = latent_mask.reshape(routed, BLK).astype(jnp.float32)
        payload = []
        for k in range(len(rank_sets)):
            send_mask = lax.dot_general(
                row_to_slot[k], mask_rows, (((0,), (0,)), ((), ())),
                preferred_element_type=jnp.float32,
            )
            send_mask = jnp.pad(send_mask, ((0, 0), (model_width, extra - BLK)))
            picked = lax.dot_general(
                token_to_slot[k], tokens_ext, (((0,), (0,)), ((), ())),
                preferred_element_type=jnp.float32,
            )
            payload.append(exchange((picked + send_mask).astype(jnp.bfloat16)))
        enc_ext = jnp.pad(enc_weight, ((0, extra), (0, 0)))

    with jax.named_scope("encode_decode"):
        col_block = jnp.arange(local_lat, dtype=jnp.int32) // BLK
        gates, codes, returned = [], [], []
        for k in range(len(rank_sets)):
            rows = payload[k].shape[0]
            row_block = jnp.arange(rows, dtype=jnp.int32) % local_blocks
            in_block = row_block[:, None] == col_block[None, :]
            mask_k = payload[k][:, model_width:model_width + BLK].astype(jnp.float32)
            gate_k = jnp.where(in_block, jnp.tile(mask_k, (1, local_blocks)), 0.0)
            preact = jnp.dot(payload[k], enc_ext, preferred_element_type=jnp.float32)
            preact = preact + enc_bias.astype(jnp.float32)[None, :]
            code_k = (preact * gate_k).astype(jnp.bfloat16)
            partials = jnp.dot(code_k, dec_weight, preferred_element_type=jnp.float32).astype(
                jnp.bfloat16
            )
            gates.append(gate_k)
            codes.append(code_k)
            returned.append(exchange(partials))

    with jax.named_scope("combine"):
        rebuilt = dec_bias.astype(jnp.float32)[None, :] - tokens.astype(jnp.float32)
        for k in range(len(rank_sets)):
            rebuilt = rebuilt + jnp.dot(
                token_to_slot[k], returned[k], preferred_element_type=jnp.float32
            )
        err_b = rebuilt.astype(jnp.bfloat16)
        error_rows = []
        for k in range(len(rank_sets)):
            send_err = pick_rows(token_to_slot[k], err_b)
            if error_rows:
                send_err = send_err + 0 * error_rows[0][:1, :1]
            error_rows.append(exchange(send_err))

    with jax.named_scope("backward"):
        enc_grad = dec_grad_t = bias_grad = 0.0
        for k in range(len(rank_sets)):
            pre_grad = lax.dot_general(
                error_rows[k], dec_weight, (((1,), (1,)), ((), ())),
                preferred_element_type=jnp.float32,
            ) * gates[k]
            pre_grad_b = pre_grad.astype(jnp.bfloat16)
            enc_grad = enc_grad + lax.dot_general(
                payload[k], pre_grad_b, (((0,), (0,)), ((), ())),
                preferred_element_type=jnp.float32,
            )[:model_width]
            dec_grad_t = dec_grad_t + lax.dot_general(
                error_rows[k], codes[k], (((0,), (0,)), ((), ())),
                preferred_element_type=jnp.float32,
            )
            bias_grad = bias_grad + jnp.sum(pre_grad, axis=0)
            if k == 0:
                enc_b, dec_b, bias_grad = lax.optimization_barrier(
                    (enc_grad.astype(jnp.bfloat16), dec_grad_t.astype(jnp.bfloat16), bias_grad)
                )
                enc_grad, dec_grad_t = enc_b.astype(jnp.float32), dec_b.astype(jnp.float32)

    with jax.named_scope("grad_reduce"):
        rows_per = model_width // n_batch
        bias_per = local_lat // n_batch
        pad_rows = 8
        weights = jnp.concatenate(
            [
                enc_grad.astype(jnp.bfloat16).reshape(n_batch, rows_per, local_lat),
                dec_grad_t.astype(jnp.bfloat16).reshape(n_batch, rows_per, local_lat),
            ],
            axis=2,
        )
        bias_block = jnp.pad(
            bias_grad.astype(jnp.bfloat16).reshape(n_batch, 1, bias_per),
            ((0, 0), (0, pad_rows - 1), (0, 2 * local_lat - bias_per)),
        )
        stacked = jnp.concatenate([weights, bias_block], axis=1).reshape(
            n_batch * (rows_per + pad_rows), 2 * local_lat
        )
        reduced = lax.psum_scatter(stacked, "batch", scatter_dimension=0, tiled=True)
        grad_enc_weight = reduced[:rows_per, :local_lat].astype(jnp.float32)
        grad_dec_weight = reduced[:rows_per, local_lat:].T.astype(jnp.float32)
        bias_share = reduced[rows_per, :bias_per].astype(jnp.float32)
    return (grad_enc_weight, bias_share, grad_dec_weight)


def solution(mesh):
    in_specs = (
        P(("loop", "inner", "batch"), None),
        P(("loop", "inner", "batch"), None),
        P(("loop", "inner", "batch"), None, None),
        P(None, ("loop", "inner")),
        P(("loop", "inner")),
        P(("loop", "inner"), None),
        P(),
    )
    out_specs = (
        P("batch", ("loop", "inner")),
        P(("loop", "inner", "batch")),
        P(("loop", "inner"), "batch"),
    )
    return jax.shard_map(shards, mesh=mesh, in_specs=in_specs, out_specs=out_specs, check_vma=False)
```

```python
import jax
import jax.numpy as jnp
from jax import lax
from jax.sharding import PartitionSpec as P

BLK = 64
OWNER_AXES = ("loop", "inner")


def exchange(rows):
    return lax.all_to_all(rows, OWNER_AXES, split_axis=0, concat_axis=0, tiled=True)


def pick_rows(select, rows):
    return lax.dot_general(
        select, rows, (((0,), (0,)), ((), ())), preferred_element_type=jnp.float32
    ).astype(rows.dtype)


def shards(tokens, block_ids, latent_mask, enc_weight, enc_bias, dec_weight, dec_bias):
    tok_dev, model_width = tokens.shape
    pick_count = block_ids.shape[1]
    local_lat = enc_weight.shape[1]
    local_blocks = local_lat // BLK
    owners = lax.axis_size("loop") * lax.axis_size("inner")
    num_blocks = local_blocks * owners
    n_batch = lax.axis_size("batch")
    capacity = (9 * tok_dev * pick_count + 8 * num_blocks - 1) // (8 * num_blocks)
    routed = tok_dev * pick_count
    main_ranks = min(capacity, (capacity * local_blocks // 8) * 8 // local_blocks)
    rank_sets = [(0, main_ranks), (main_ranks, capacity)] if main_ranks < capacity else [(0, capacity)]
    extra = 2 * BLK

    with jax.named_scope("slot_tables"):
        flat_ids = block_ids.reshape(routed)
        row_pos = jnp.arange(routed, dtype=jnp.int32)
        earlier_same = (flat_ids[:, None] == flat_ids[None, :]) & (row_pos[None, :] < row_pos[:, None])
        slot_rank = jnp.sum(earlier_same.astype(jnp.int32), axis=1)
        owner_of = flat_ids // local_blocks
        local_of = flat_ids % local_blocks
        row_to_slot, token_to_slot = [], []
        for lo, hi in rank_sets:
            per_owner = (hi - lo) * local_blocks
            target = owner_of * per_owner + (slot_rank - lo) * local_blocks + local_of
            target = jnp.where((slot_rank >= lo) & (slot_rank < hi), target, -1)
            hit = target[:, None] == jnp.arange(owners * per_owner, dtype=jnp.int32)[None, :]
            row_to_slot.append(hit.astype(jnp.bfloat16))
            token_to_slot.append(
                jnp.sum(hit.reshape(tok_dev, pick_count, -1).astype(jnp.int32), axis=1).astype(
                    jnp.bfloat16
                )
            )

    with jax.named_scope("dispatch"):
        tokens_ext = jnp.pad(tokens, ((0, 0), (0, extra)))
        mask_rows = latent_mask.reshape(routed, BLK).astype(jnp.float32)
        payload = []
        for k in range(len(rank_sets)):
            send_mask = lax.dot_general(
                row_to_slot[k], mask_rows, (((0,), (0,)), ((), ())),
                preferred_element_type=jnp.float32,
            )
            send_mask = jnp.pad(send_mask, ((0, 0), (model_width, extra - BLK)))
            picked = lax.dot_general(
                token_to_slot[k], tokens_ext, (((0,), (0,)), ((), ())),
                preferred_element_type=jnp.float32,
            )
            payload.append(exchange((picked + send_mask).astype(jnp.bfloat16)))
        enc_ext = jnp.pad(enc_weight, ((0, extra), (0, 0)))

    with jax.named_scope("encode_decode"):
        col_block = jnp.arange(local_lat, dtype=jnp.int32) // BLK
        gates, codes, returned = [], [], []
        for k in range(len(rank_sets)):
            rows = payload[k].shape[0]
            row_block = jnp.arange(rows, dtype=jnp.int32) % local_blocks
            in_block = row_block[:, None] == col_block[None, :]
            mask_k = payload[k][:, model_width:model_width + BLK].astype(jnp.float32)
            gate_k = jnp.where(in_block, jnp.tile(mask_k, (1, local_blocks)), 0.0)
            preact = jnp.dot(payload[k], enc_ext, preferred_element_type=jnp.float32)
            preact = preact + enc_bias.astype(jnp.float32)[None, :]
            code_k = (preact * gate_k).astype(jnp.bfloat16)
            partials = jnp.dot(code_k, dec_weight, preferred_element_type=jnp.float32).astype(
                jnp.bfloat16
            )
            gates.append(gate_k)
            codes.append(code_k)
            returned.append(exchange(partials))

    with jax.named_scope("combine"):
        rebuilt = dec_bias.astype(jnp.float32)[None, :] - tokens.astype(jnp.float32)
        for k in range(len(rank_sets)):
            rebuilt = rebuilt + jnp.dot(
                token_to_slot[k], returned[k], preferred_element_type=jnp.float32
            )
        err_b = rebuilt.astype(jnp.bfloat16)
        error_rows = []
        for k in range(len(rank_sets)):
            send_err = pick_rows(token_to_slot[k], err_b)
            if error_rows:
                send_err = send_err + 0 * error_rows[0][:1, :1]
            if error_rows:
                send_err = send_err.reshape(owners, -1, model_width)
            error_rows.append(exchange(send_err))

    with jax.named_scope("backward"):
        enc_grad = dec_grad_t = bias_grad = 0.0
        for k in range(len(rank_sets)):
            err_k = error_rows[k]
            lead = err_k.shape[:-1]
            rows_k = tuple(range(len(lead)))
            pre_grad = lax.dot_general(
                err_k, dec_weight, (((len(lead),), (1,)), ((), ())),
                preferred_element_type=jnp.float32,
            ) * gates[k].reshape(lead + (local_lat,))
            pre_grad_b = pre_grad.astype(jnp.bfloat16)
            enc_grad = enc_grad + lax.dot_general(
                payload[k].reshape(lead + (-1,)), pre_grad_b, ((rows_k, rows_k), ((), ())),
                preferred_element_type=jnp.float32,
            )[:model_width]
            dec_grad_t = dec_grad_t + lax.dot_general(
                err_k, codes[k].reshape(lead + (local_lat,)), ((rows_k, rows_k), ((), ())),
                preferred_element_type=jnp.float32,
            )
            bias_grad = bias_grad + jnp.sum(pre_grad, axis=rows_k)
            if k == 0:
                enc_b, dec_b, bias_grad = lax.optimization_barrier(
                    (enc_grad.astype(jnp.bfloat16), dec_grad_t.astype(jnp.bfloat16), bias_grad)
                )
                enc_grad, dec_grad_t = enc_b.astype(jnp.float32), dec_b.astype(jnp.float32)

    with jax.named_scope("grad_reduce"):
        rows_per = model_width // n_batch
        bias_per = local_lat // n_batch
        pad_rows = 8
        weights = jnp.concatenate(
            [
                enc_grad.astype(jnp.bfloat16).reshape(n_batch, rows_per, local_lat),
                dec_grad_t.astype(jnp.bfloat16).reshape(n_batch, rows_per, local_lat),
            ],
            axis=2,
        )
        bias_block = jnp.pad(
            bias_grad.astype(jnp.bfloat16).reshape(n_batch, 1, bias_per),
            ((0, 0), (0, pad_rows - 1), (0, 2 * local_lat - bias_per)),
        )
        stacked = jnp.concatenate([weights, bias_block], axis=1).reshape(
            n_batch * (rows_per + pad_rows), 2 * local_lat
        )
        reduced = lax.psum_scatter(stacked, "batch", scatter_dimension=0, tiled=True).astype(
            jnp.float32
        )
        grad_enc_weight = reduced[:rows_per, :local_lat]
        grad_dec_weight = reduced[:rows_per, local_lat:].T
        bias_share = reduced[rows_per, :bias_per]
    return (grad_enc_weight, bias_share, grad_dec_weight)


def solution(mesh):
    in_specs = (
        P(("loop", "inner", "batch"), None),
        P(("loop", "inner", "batch"), None),
        P(("loop", "inner", "batch"), None, None),
        P(None, ("loop", "inner")),
        P(("loop", "inner")),
        P(("loop", "inner"), None),
        P(),
    )
    out_specs = (
        P("batch", ("loop", "inner")),
        P(("loop", "inner", "batch")),
        P(("loop", "inner"), "batch"),
    )
    return jax.shard_map(shards, mesh=mesh, in_specs=in_specs, out_specs=out_specs, check_vma=False)
```
